32 devices in a mesh: grp: 2 (over y), freq: 4 (over z), rcv: 2 (over x), sub: 2 (over core).
Axes of the slice: x: 2, y: 2, z: 4, core: 2. Of those that a mesh axis runs over, the one named last changes fastest.
Arguments:
- reflection: float32 [4, 16, 512, 512], P('grp', 'freq', None, 'rcv'), parts along dimension 0, may hold values from -0.25 to 0.25
- focus: float32 [32, 2, 128, 512], P(('grp', 'freq'), None, 'sub', 'rcv'), parts along dimension 0, may hold values from -6 to 6
- initial: float32 [32, 2, 128, 512], P(('grp', 'freq'), None, 'sub', 'rcv'), parts along dimension 0, may hold values from -6 to 6
- onset: int32 [256, 512], P(('grp', 'sub')), parts along dimension 0, may hold values from 64 to 511
Outputs:
- updated: float32 [32, 2, 128, 512], P(('grp', 'freq'), None, 'sub', 'rcv'), parts along dimension 0
The draws below stay inside these ranges and needn't reach their ends.
There are 2 independent parts, one for each index of `grp`. The reference program is written for one: setup_inputs(seed, part) draws one part's arguments, and reference() takes and returns one part's arrays. A program takes and returns all parts, laid end to end along the dimension named above; each array names one. Nothing has to cross between parts.
All inputs are finite; a program needn't handle non-finite values.
Results may differ from the reference program's by a relative error of at most 0.00005.
Values sent between devices are 32-bit elements; how exact they have to be, the bound alone decides.
No kernel may reach another device: no remote copies, remote signals or barrier semaphores. Data moves between devices by JAX's collectives and lax.ppermute only.
A program may use at most 64 MiB of HBM per device.

```python
import math
import jax
import jax.numpy as jnp
from jax import lax

NT = 512
NV = 128
NS = 512
NF = 16
NR = 512


def with_ends(values, key, smallest, top_value):
    extent = values.shape
    spot = [jax.random.randint(jax.random.fold_in(key, axis), (), 0, extent[axis]) for axis in range(len(extent))]
    values = values.at[tuple(spot)].set(smallest)
    longest = extent.index(max(extent))
    spot[longest] = (spot[longest] + 1) % extent[longest]
    return values.at[tuple(spot)].set(top_value)


def block_scale(rng, dims, shards, low, top_value):
    def one(dim, parts):
        steps = jax.random.uniform(jax.random.fold_in(jax.random.fold_in(rng, 6), dim), (parts,), jnp.float32, low / len(shards), top_value / len(shards))
        return jnp.repeat(jnp.exp(steps), dims[dim] // parts).reshape((-1,) + (1,) * (len(dims) - dim - 1))

    gain = one(*shards[0])
    for cut in shards[1:]:
        gain = gain * one(*cut)
    return gain


def centred(stream_key, dims, spread, limit, split=(), kind=jnp.bfloat16):
    values = spread * jax.random.normal(stream_key, dims, jnp.float32)
    if split:
        values = values * block_scale(stream_key, dims, split, -0.22, 0.18)
    return jnp.clip(values, -limit, limit).astype(kind)


def setup_inputs(seed: int = 0, part: int = 0) -> dict:
    streams_of = jax.random.split(jax.random.key(seed), 5)
    own_keys = jax.random.split(jax.random.fold_in(streams_of[4], part), 5)
    return {
        "reflection": centred(own_keys[0], (2, NF, NS, NR), NR ** -0.5, 0.25, ((1, 4), (3, 2)), jnp.float32),
        "focus": centred(own_keys[1], (NF, 2, NV, NR), 1.0, 6.0, ((0, 4), (2, 2), (3, 2)), jnp.float32),
        "initial": centred(own_keys[2], (NF, 2, NV, NR), 1.0, 6.0, ((0, 4), (2, 2), (3, 2)), jnp.float32),
        "onset": with_ends(jax.random.randint(own_keys[3], (NV, NS), NT // 8, NT), jax.random.fold_in(own_keys[3], 1), NT // 8, NT - 1).astype(jnp.int32),
    }


def tables(count):
    bins = jnp.arange(1, count + 1, dtype=jnp.int32)
    samples = jnp.arange(NT, dtype=jnp.int32)
    phase = ((bins[:, None] * samples[None, :]) % NT).astype(jnp.float32) * (2.0 * math.pi / NT)
    return jnp.cos(phase), jnp.sin(phase)


def reference(reflection, focus, initial, onset):
    upper_limit = lax.Precision.HIGHEST
    reflection_real, reflection_imaginary = reflection[0], reflection[1]
    focusing_real, focusing_imaginary = focus[:, 0], focus[:, 1]
    product_real = jnp.einsum("dah,dph->adp", reflection_real, focusing_real, precision=upper_limit) - jnp.einsum("dah,dph->adp", reflection_imaginary, focusing_imaginary, precision=upper_limit)
    product_imaginary = jnp.einsum("dah,dph->adp", reflection_real, focusing_imaginary, precision=upper_limit) + jnp.einsum("dah,dph->adp", reflection_imaginary, focusing_real, precision=upper_limit)
    cosine, sine = tables(NF)
    trace = (2.0 / NT) * (jnp.einsum("sfv,ft->svt", product_real, cosine, precision=upper_limit) - jnp.einsum("sfv,ft->svt", product_imaginary, sine, precision=upper_limit))
    samples = jnp.arange(NT, dtype=jnp.int32)
    keep = samples[None, None, :] < jnp.transpose(onset)[:, :, None]
    windowed = jnp.where(keep, trace, jnp.float32(0.0))
    backward_real = jnp.einsum("svt,ft->sfv", windowed, cosine, precision=upper_limit)
    backward_imaginary = -jnp.einsum("svt,ft->sfv", windowed, sine, precision=upper_limit)
    adjoint_real = jnp.einsum("jnb,njg->jgb", reflection_real, backward_real, precision=upper_limit) + jnp.einsum("jnb,njg->jgb", reflection_imaginary, backward_imaginary, precision=upper_limit)
    adjoint_imaginary = jnp.einsum("jnb,njg->jgb", reflection_real, backward_imaginary, precision=upper_limit) - jnp.einsum("jnb,njg->jgb", reflection_imaginary, backward_real, precision=upper_limit)
    return initial + jnp.stack([adjoint_real, adjoint_imaginary], axis=1)
```

```python
import math

import jax
import jax.numpy as jnp
import numpy as np
from jax import lax
from jax.experimental import pallas as pl
from jax.experimental.pallas import tpu as pltpu
from jax.sharding import PartitionSpec as P

NT = 512
HIGHEST = lax.Precision.HIGHEST


def bases(nfreq):
    bins = np.arange(1, nfreq + 1, dtype=np.int64)
    samples = np.arange(NT, dtype=np.int64)
    phase = (bins[:, None] * samples[None, :] % NT).astype(np.float64) * (2.0 * math.pi / NT)
    cosine, sine = np.cos(phase), np.sin(phase)
    fwd = (2.0 / NT) * np.concatenate([cosine, -sine], axis=0).T
    bwd = np.concatenate([cosine, -sine], axis=0)
    return jnp.asarray(fwd.astype(np.float32)), jnp.asarray(bwd.astype(np.float32))


def window_kernel(spec_ref, onset_ref, fwd_ref, bwd_ref, out_ref):
    trace = jnp.dot(fwd_ref[...], spec_ref[...], precision=HIGHEST, preferred_element_type=jnp.float32)
    samples = lax.broadcasted_iota(jnp.int32, trace.shape, 0)
    windowed = jnp.where(samples < onset_ref[...], trace, jnp.float32(0.0))
    out_ref[...] = jnp.dot(bwd_ref[...], windowed, precision=HIGHEST, preferred_element_type=jnp.float32)


def window_traces(spec, onset_row):
    k2, rows = spec.shape
    fwd, bwd = bases(k2 // 2)
    tile = min(rows, 1024)
    return pl.pallas_call(
        window_kernel,
        out_shape=jax.ShapeDtypeStruct((k2, rows), jnp.float32),
        grid=(rows // tile,),
        in_specs=[
            pl.BlockSpec((k2, tile), lambda i: (0, i)),
            pl.BlockSpec((1, tile), lambda i: (0, i)),
            pl.BlockSpec((NT, k2), lambda i: (0, 0)),
            pl.BlockSpec((k2, NT), lambda i: (0, 0)),
        ],
        out_specs=pl.BlockSpec((k2, tile), lambda i: (0, i)),
        cost_estimate=pl.CostEstimate(
            flops=4 * NT * k2 * rows * 6, transcendentals=0, bytes_accessed=(2 * k2 + 1) * rows * 4
        ),
    )(spec, onset_row, fwd, bwd)


def product_chunk(refl_real, refl_imag, focus_stack, chunk, size):
    vdev = focus_stack.shape[1] // 2
    rr = lax.dynamic_slice_in_dim(refl_real, chunk * size, size, axis=1)
    ri = lax.dynamic_slice_in_dim(refl_imag, chunk * size, size, axis=1)
    a = jnp.einsum("fsr,fwr->fsw", rr, focus_stack, precision=HIGHEST)
    b = jnp.einsum("fsr,fwr->fsw", ri, focus_stack, precision=HIGHEST)
    real = a[..., :vdev] - b[..., vdev:]
    imag = a[..., vdev:] + b[..., :vdev]
    return jnp.stack([real, imag], axis=0)


def adjoint_chunk(refl_real, refl_imag, back, chunk):
    _, fdev, size, vdev = back.shape
    stacked = jnp.concatenate([back[0], back[1]], axis=-1)
    rr = lax.dynamic_slice_in_dim(refl_real, chunk * size, size, axis=1)
    ri = lax.dynamic_slice_in_dim(refl_imag, chunk * size, size, axis=1)
    g_r = jnp.einsum("fsr,fsw->fwr", rr, stacked, precision=HIGHEST)
    g_i = jnp.einsum("fsr,fsw->fwr", ri, stacked, precision=HIGHEST)
    real = g_r[:, :vdev] + g_i[:, vdev:]
    imag = g_r[:, vdev:] - g_i[:, :vdev]
    return jnp.stack([real, imag], axis=1)


def per_device(reflection, focus, initial, onset):
    refl_real, refl_imag = reflection[0], reflection[1]
    fdev, total_src, nrcv_local = refl_real.shape
    vdev = focus.shape[2]
    focus_stack = focus.reshape(fdev, 2 * vdev, nrcv_local)
    n_rcv = lax.axis_size("rcv")
    n_freq = lax.axis_size("freq")
    me_rcv = lax.axis_index("rcv")
    me_freq = lax.axis_index("freq")
    own = total_src // n_rcv
    width = own // n_freq

    summed = None
    for shift in range(n_rcv):
        dest = (me_rcv + shift) % n_rcv
        part = product_chunk(refl_real, refl_imag, focus_stack, dest, own)
        if shift:
            part = lax.ppermute(part, "rcv", [(i, (i + shift) % n_rcv) for i in range(n_rcv)])
        summed = part if summed is None else summed + part

    spectra = lax.all_to_all(summed, "freq", split_axis=2, concat_axis=1, tiled=True)
    nfreq = spectra.shape[1]
    start = me_rcv * own + me_freq * width
    onset_part = lax.dynamic_slice_in_dim(onset, start, width, axis=1)
    onset_row = jnp.transpose(onset_part).reshape(1, width * vdev)
    back = window_traces(spectra.reshape(2 * nfreq, width * vdev), onset_row)
    back = back.reshape(2, nfreq, width, vdev)
    back = lax.all_to_all(back, "freq", split_axis=1, concat_axis=2, tiled=True)

    adjoint = None
    for shift in range(n_rcv):
        piece = back
        if shift:
            piece = lax.ppermute(back, "rcv", [(i, (i + shift) % n_rcv) for i in range(n_rcv)])
        term = adjoint_chunk(refl_real, refl_imag, piece, (me_rcv - shift) % n_rcv)
        adjoint = term if adjoint is None else adjoint + term
    return initial + adjoint


def solution(mesh):
    return jax.shard_map(
        per_device,
        mesh=mesh,
        in_specs=(
            P("grp", "freq", None, "rcv"),
            P(("grp", "freq"), None, "sub", "rcv"),
            P(("grp", "freq"), None, "sub", "rcv"),
            P(("grp", "sub"), None),
        ),
        out_specs=P(("grp", "freq"), None, "sub", "rcv"),
        check_vma=False,
    )
```

```python
import math

import jax
import jax.numpy as jnp
import numpy as np
from jax import lax
from jax.experimental import pallas as pl
from jax.experimental.pallas import tpu as pltpu
from jax.sharding import PartitionSpec as P

NT = 512
HIGH = lax.Precision.HIGH


def bases(n_freq_dev, fdev):
    bins = np.arange(1, n_freq_dev * fdev + 1, dtype=np.int64)
    samples = np.arange(NT, dtype=np.int64)
    phase = (bins[:, None] * samples[None, :] % NT).astype(np.float64) * (2.0 * math.pi / NT)
    cosine, sine = np.cos(phase), np.sin(phase)
    pair = np.stack([cosine, -sine], axis=1).reshape(n_freq_dev, fdev * 2, NT)
    fwd = (2.0 / NT) * pair
    return jnp.asarray(fwd.astype(np.float32)), jnp.asarray(pair.astype(np.float32))


def window_kernel(x_ref, onset_ref, fwd_t_ref, bwd_ref, out_ref):
    fwd_t = fwd_t_ref[...]
    bwd = bwd_ref[...]
    for v in range(x_ref.shape[1]):
        trace = jnp.dot(fwd_t, x_ref[:, v, :], precision=HIGH, preferred_element_type=jnp.float32)
        samples = lax.broadcasted_iota(jnp.int32, trace.shape, 0)
        windowed = jnp.where(samples < onset_ref[pl.ds(v, 1), :], trace, jnp.float32(0.0))
        out_ref[:, v, :] = jnp.dot(bwd, windowed, precision=HIGH, preferred_element_type=jnp.float32)


def window_traces(spec, onset_part, fwd_t, bwd):
    k2, nv, ns = spec.shape
    vt = 8 if nv % 8 == 0 else nv
    return pl.pallas_call(
        window_kernel,
        out_shape=jax.ShapeDtypeStruct((k2, nv, ns), jnp.float32),
        grid=(nv // vt,),
        in_specs=[
            pl.BlockSpec((k2, vt, ns), lambda i: (0, i, 0)),
            pl.BlockSpec((vt, ns), lambda i: (i, 0)),
            pl.BlockSpec((NT, k2), lambda i: (0, 0)),
            pl.BlockSpec((k2, NT), lambda i: (0, 0)),
        ],
        out_specs=pl.BlockSpec((k2, vt, ns), lambda i: (0, i, 0)),
        cost_estimate=pl.CostEstimate(
            flops=4 * NT * k2 * nv * ns * 3, transcendentals=0, bytes_accessed=(2 * k2 + 1) * nv * ns * 4
        ),
    )(spec, onset_part, fwd_t, bwd)


def product_chunk(refl_real, refl_imag, focus_stack, chunk, size):
    vdev = focus_stack.shape[1] // 2
    rr = lax.dynamic_slice_in_dim(refl_real, chunk * size, size, axis=1)
    ri = lax.dynamic_slice_in_dim(refl_imag, chunk * size, size, axis=1)
    a = jnp.einsum("fwr,fsr->fws", focus_stack, rr, precision=HIGH)
    b = jnp.einsum("fwr,fsr->fws", focus_stack, ri, precision=HIGH)
    real = a[:, :vdev] - b[:, vdev:]
    imag = a[:, vdev:] + b[:, :vdev]
    return jnp.stack([real, imag], axis=1)


def adjoint_chunk(refl_real, refl_imag, back, chunk):
    fdev, _, vdev, size = back.shape
    stacked = back.reshape(fdev, 2 * vdev, size)
    rr = lax.dynamic_slice_in_dim(refl_real, chunk * size, size, axis=1)
    ri = lax.dynamic_slice_in_dim(refl_imag, chunk * size, size, axis=1)
    g_r = jnp.einsum("fws,fsr->fwr", stacked, rr, precision=HIGH)
    g_i = jnp.einsum("fws,fsr->fwr", stacked, ri, precision=HIGH)
    real = g_r[:, :vdev] + g_i[:, vdev:]
    imag = g_r[:, vdev:] - g_i[:, :vdev]
    return jnp.stack([real, imag], axis=1)


def shifted(x, axis, shift, n):
    return lax.ppermute(x, axis, [(i, (i + shift) % n) for i in range(n)])


def per_device(reflection, focus, initial, onset):
    refl_real, refl_imag = reflection[0], reflection[1]
    fdev, total_src, nrcv_local = refl_real.shape
    vdev = focus.shape[2]
    focus_stack = focus.reshape(fdev, 2 * vdev, nrcv_local)
    n_rcv = lax.axis_size("rcv")
    n_freq = lax.axis_size("freq")
    me_rcv = lax.axis_index("rcv")
    me_freq = lax.axis_index("freq")
    own = total_src // n_rcv
    vc = vdev // n_freq

    summed = None
    for shift in range(n_rcv):
        part = product_chunk(refl_real, refl_imag, focus_stack, (me_rcv + shift) % n_rcv, own)
        if shift:
            part = shifted(part, "rcv", shift, n_rcv)
        summed = part if summed is None else summed + part

    blocks = []
    for shift in range(n_freq):
        dest = (me_freq + shift) % n_freq
        block = lax.dynamic_slice_in_dim(summed, dest * vc, vc, axis=2)
        if shift:
            block = shifted(block, "freq", shift, n_freq)
        blocks.append(block)
    spec = jnp.stack(blocks, axis=0).reshape(n_freq * fdev * 2, vc, own)
    fwd, bwd = bases(n_freq, fdev)
    order = (me_freq - jnp.arange(n_freq)) % n_freq
    fwd_t = jnp.take(fwd, order, axis=0).reshape(n_freq * fdev * 2, NT).T
    bwd = jnp.take(bwd, order, axis=0).reshape(n_freq * fdev * 2, NT)
    onset_part = lax.dynamic_slice(onset, (me_freq * vc, me_rcv * own), (vc, own))
    back = window_traces(spec, onset_part, fwd_t, bwd).reshape(n_freq, fdev, 2, vc, own)

    back_full = jnp.zeros((fdev, 2, vdev, own), jnp.float32)
    for shift in range(n_freq):
        piece = back[shift]
        if shift:
            piece = shifted(piece, "freq", n_freq - shift, n_freq)
        src = (me_freq + shift) % n_freq
        back_full = lax.dynamic_update_slice_in_dim(back_full, piece, src * vc, axis=2)

    adjoint = None
    for shift in range(n_rcv):
        piece = back_full
        if shift:
            piece = shifted(back_full, "rcv", shift, n_rcv)
        term = adjoint_chunk(refl_real, refl_imag, piece, (me_rcv - shift) % n_rcv)
        adjoint = term if adjoint is None else adjoint + term
    return initial + adjoint


def solution(mesh):
    return jax.shard_map(
        per_device,
        mesh=mesh,
        in_specs=(
            P("grp", "freq", None, "rcv"),
            P(("grp", "freq"), None, "sub", "rcv"),
            P(("grp", "freq"), None, "sub", "rcv"),
            P(("grp", "sub"), None),
        ),
        out_specs=P(("grp", "freq"), None, "sub", "rcv"),
        check_vma=False,
    )
```

```python
import math

import jax
import jax.numpy as jnp
import numpy as np
from jax import lax
from jax.experimental import pallas as pl
from jax.experimental.pallas import tpu as pltpu
from jax.sharding import PartitionSpec as P

NT = 512
HIGH = lax.Precision.HIGH
HIGHEST = lax.Precision.HIGHEST


def bases(n_freq_dev, fdev):
    bins = np.arange(1, n_freq_dev * fdev + 1, dtype=np.int64)
    samples = np.arange(NT, dtype=np.int64)
    phase = (bins[:, None] * samples[None, :] % NT).astype(np.float64) * (2.0 * math.pi / NT)
    cosine, sine = np.cos(phase), np.sin(phase)
    pair = np.stack([cosine, -sine], axis=1).reshape(n_freq_dev, fdev * 2, NT)
    fwd = (2.0 / NT) * pair
    return jnp.asarray(fwd.astype(np.float32)), jnp.asarray(pair.astype(np.float32))


def window_kernel(x_ref, onset_ref, fwd_t_ref, bwd_ref, out_ref):
    fwd_t = fwd_t_ref[...]
    bwd = bwd_ref[...]
    for v in range(x_ref.shape[1]):
        trace = jnp.dot(fwd_t, x_ref[:, v, :], precision=HIGHEST, preferred_element_type=jnp.float32)
        samples = lax.broadcasted_iota(jnp.int32, trace.shape, 0)
        windowed = jnp.where(samples < onset_ref[pl.ds(v, 1), :], trace, jnp.float32(0.0))
        out_ref[:, v, :] = jnp.dot(bwd, windowed, precision=HIGHEST, preferred_element_type=jnp.float32)


def window_traces(spec, onset_part, fwd_t, bwd):
    k2, nv, ns = spec.shape
    vt = 8 if nv % 8 == 0 else nv
    return pl.pallas_call(
        window_kernel,
        out_shape=jax.ShapeDtypeStruct((k2, nv, ns), jnp.float32),
        grid=(nv // vt,),
        in_specs=[
            pl.BlockSpec((k2, vt, ns), lambda i: (0, i, 0)),
            pl.BlockSpec((vt, ns), lambda i: (i, 0)),
            pl.BlockSpec((NT, k2), lambda i: (0, 0)),
            pl.BlockSpec((k2, NT), lambda i: (0, 0)),
        ],
        out_specs=pl.BlockSpec((k2, vt, ns), lambda i: (0, i, 0)),
        cost_estimate=pl.CostEstimate(
            flops=4 * NT * k2 * nv * ns * 6, transcendentals=0, bytes_accessed=(2 * k2 + 1) * nv * ns * 4
        ),
    )(spec, onset_part, fwd_t, bwd)


def product_chunk(reflection, focus_stack, chunk, size):
    vdev = focus_stack.shape[1] // 2
    refl = lax.dynamic_slice_in_dim(reflection, chunk * size, size, axis=2)
    ab = jnp.einsum("fwr,cfsr->fcws", focus_stack, refl, precision=HIGH)
    a, b = ab[:, 0], ab[:, 1]
    real = a[:, :vdev] - b[:, vdev:]
    imag = a[:, vdev:] + b[:, :vdev]
    return jnp.stack([real, imag], axis=1)


def adjoint_chunk(reflection, back, chunk):
    fdev, _, vdev, size = back.shape
    stacked = back.reshape(fdev, 2 * vdev, size)
    refl = lax.dynamic_slice_in_dim(reflection, chunk * size, size, axis=2)
    g = jnp.einsum("fws,cfsr->fcwr", stacked, refl, precision=HIGH)
    g_r, g_i = g[:, 0], g[:, 1]
    real = g_r[:, :vdev] + g_i[:, vdev:]
    imag = g_r[:, vdev:] - g_i[:, :vdev]
    return jnp.stack([real, imag], axis=1)


def shifted(x, axis, shift, n):
    return lax.ppermute(x, axis, [(i, (i + shift) % n) for i in range(n)])


def per_device(reflection, focus, initial, onset):
    _, fdev, total_src, nrcv_local = reflection.shape
    vdev = focus.shape[2]
    focus_stack = focus.reshape(fdev, 2 * vdev, nrcv_local)
    n_rcv = lax.axis_size("rcv")
    n_freq = lax.axis_size("freq")
    me_rcv = lax.axis_index("rcv")
    me_freq = lax.axis_index("freq")
    own = total_src // n_rcv
    vc = vdev // n_freq

    summed = None
    for shift in range(n_rcv):
        part = product_chunk(reflection, focus_stack, (me_rcv + shift) % n_rcv, own)
        if shift:
            part = shifted(part, "rcv", shift, n_rcv)
        summed = part if summed is None else summed + part

    blocks = []
    for shift in range(n_freq):
        dest = (me_freq + shift) % n_freq
        block = lax.dynamic_slice_in_dim(summed, dest * vc, vc, axis=2)
        if shift:
            block = shifted(block, "freq", shift, n_freq)
        blocks.append(block)
    spec = jnp.stack(blocks, axis=0).reshape(n_freq * fdev * 2, vc, own)
    fwd, bwd = bases(n_freq, fdev)
    order = (me_freq - jnp.arange(n_freq)) % n_freq
    fwd_t = jnp.take(fwd, order, axis=0).reshape(n_freq * fdev * 2, NT).T
    bwd = jnp.take(bwd, order, axis=0).reshape(n_freq * fdev * 2, NT)
    onset_part = lax.dynamic_slice(onset, (me_freq * vc, me_rcv * own), (vc, own))
    back = window_traces(spec, onset_part, fwd_t, bwd).reshape(n_freq, fdev, 2, vc, own)

    back_full = jnp.zeros((fdev, 2, vdev, own), jnp.float32)
    for shift in range(n_freq):
        piece = back[shift]
        if shift:
            piece = shifted(piece, "freq", n_freq - shift, n_freq)
        src = (me_freq + shift) % n_freq
        back_full = lax.dynamic_update_slice_in_dim(back_full, piece, src * vc, axis=2)

    adjoint = None
    for shift in range(n_rcv):
        piece = back_full
        if shift:
            piece = shifted(back_full, "rcv", shift, n_rcv)
        term = adjoint_chunk(reflection, piece, (me_rcv - shift) % n_rcv)
        adjoint = term if adjoint is None else adjoint + term
    return initial + adjoint


def solution(mesh):
    return jax.shard_map(
        per_device,
        mesh=mesh,
        in_specs=(
            P("grp", "freq", None, "rcv"),
            P(("grp", "freq"), None, "sub", "rcv"),
            P(("grp", "freq"), None, "sub", "rcv"),
            P(("grp", "sub"), None),
        ),
        out_specs=P(("grp", "freq"), None, "sub", "rcv"),
        check_vma=False,
    )
```

```python
import math

import jax
import jax.numpy as jnp
import numpy as np
from jax import lax
from jax.experimental import pallas as pl
from jax.experimental.pallas import tpu as pltpu
from jax.sharding import PartitionSpec as P

NT = 512
BF16 = jnp.bfloat16


def split(x):
    high = x.astype(BF16)
    return high, (x - high.astype(jnp.float32)).astype(BF16)


def split_xla(x):
    high = lax.reduce_precision(x, exponent_bits=8, mantissa_bits=7)
    return high.astype(BF16), (x - high).astype(BF16)


def dot3(eq, a, b):
    (a_hi, a_lo), (b_hi, b_lo) = a, b
    one = lambda x, y: jnp.einsum(eq, x, y, preferred_element_type=jnp.float32)
    return one(a_hi, b_hi) + (one(a_hi, b_lo) + one(a_lo, b_hi))


def bases(n_freq_dev, fdev):
    bins = np.arange(1, n_freq_dev * fdev + 1, dtype=np.int64)
    samples = np.arange(NT, dtype=np.int64)
    phase = (bins[:, None] * samples[None, :] % NT).astype(np.float64) * (2.0 * math.pi / NT)
    cosine, sine = np.cos(phase), np.sin(phase)
    pair = np.stack([cosine, -sine], axis=1).reshape(n_freq_dev, fdev * 2, NT)
    fwd = ((2.0 / NT) * pair).astype(np.float32)
    bwd = pair.astype(np.float32)
    return [jnp.asarray(x) for x in split_np(fwd) + split_np(bwd)]


def split_np(x):
    high = x.astype(BF16)
    return [high, (x - high.astype(np.float32)).astype(BF16)]


def window_kernel(x_ref, onset_ref, fwd_hi_ref, fwd_lo_ref, bwd_hi_ref, bwd_lo_ref, out_ref):
    fwd = (fwd_hi_ref[...], fwd_lo_ref[...])
    bwd = (bwd_hi_ref[...], bwd_lo_ref[...])
    for v in range(x_ref.shape[1]):
        trace = dot3("tk,ks->ts", fwd, split(x_ref[:, v, :]))
        samples = lax.broadcasted_iota(jnp.int32, trace.shape, 0)
        windowed = jnp.where(samples < onset_ref[pl.ds(v, 1), :], trace, jnp.float32(0.0))
        out_ref[:, v, :] = dot3("kt,ts->ks", bwd, split(windowed))


def window_traces(spec, onset_part, fwd_hi, fwd_lo, bwd_hi, bwd_lo):
    k2, nv, ns = spec.shape
    vt = 8 if nv % 8 == 0 else nv
    return pl.pallas_call(
        window_kernel,
        out_shape=jax.ShapeDtypeStruct((k2, nv, ns), jnp.float32),
        grid=(nv // vt,),
        in_specs=[
            pl.BlockSpec((k2, vt, ns), lambda i: (0, i, 0)),
            pl.BlockSpec((vt, ns), lambda i: (i, 0)),
            pl.BlockSpec((NT, k2), lambda i: (0, 0)),
            pl.BlockSpec((NT, k2), lambda i: (0, 0)),
            pl.BlockSpec((k2, NT), lambda i: (0, 0)),
            pl.BlockSpec((k2, NT), lambda i: (0, 0)),
        ],
        out_specs=pl.BlockSpec((k2, vt, ns), lambda i: (0, i, 0)),
        cost_estimate=pl.CostEstimate(
            flops=4 * NT * k2 * nv * ns * 3, transcendentals=0, bytes_accessed=(2 * k2 + 1) * nv * ns * 4
        ),
    )(spec, onset_part, fwd_hi, fwd_lo, bwd_hi, bwd_lo)


def product_chunk(refl_parts, focus_parts, chunk, size):
    vdev = focus_parts[0].shape[1] // 2
    refl = [lax.dynamic_slice_in_dim(x, chunk * size, size, axis=2) for x in refl_parts]
    ab = dot3("fwr,cfsr->fcws", focus_parts, refl)
    a, b = ab[:, 0], ab[:, 1]
    real = a[:, :vdev] - b[:, vdev:]
    imag = a[:, vdev:] + b[:, :vdev]
    return jnp.stack([real, imag], axis=1)


def adjoint_chunk(refl_parts, back, chunk):
    fdev, _, vdev, size = back.shape
    stacked = back.reshape(fdev, 2 * vdev, size)
    refl = [lax.dynamic_slice_in_dim(x, chunk * size, size, axis=2) for x in refl_parts]
    g = dot3("fws,cfsr->fcwr", split_xla(stacked), refl)
    g_r, g_i = g[:, 0], g[:, 1]
    real = g_r[:, :vdev] + g_i[:, vdev:]
    imag = g_r[:, vdev:] - g_i[:, :vdev]
    return jnp.stack([real, imag], axis=1)


def shifted(x, axis, shift, n):
    return lax.ppermute(x, axis, [(i, (i + shift) % n) for i in range(n)])


def per_device(reflection, focus, initial, onset):
    _, fdev, total_src, nrcv_local = reflection.shape
    vdev = focus.shape[2]
    focus_parts = split_xla(focus.reshape(fdev, 2 * vdev, nrcv_local))
    refl_parts = split_xla(reflection)
    n_rcv = lax.axis_size("rcv")
    n_freq = lax.axis_size("freq")
    me_rcv = lax.axis_index("rcv")
    me_freq = lax.axis_index("freq")
    own = total_src // n_rcv
    vc = vdev // n_freq

    summed = None
    for shift in range(n_rcv):
        part = product_chunk(refl_parts, focus_parts, (me_rcv + shift) % n_rcv, own)
        if shift:
            part = shifted(part, "rcv", shift, n_rcv)
        summed = part if summed is None else summed + part

    blocks = []
    for shift in range(n_freq):
        dest = (me_freq + shift) % n_freq
        block = lax.dynamic_slice_in_dim(summed, dest * vc, vc, axis=2)
        if shift:
            block = shifted(block, "freq", shift, n_freq)
        blocks.append(block)
    spec = jnp.stack(blocks, axis=0).reshape(n_freq * fdev * 2, vc, own)
    order = (me_freq - jnp.arange(n_freq)) % n_freq
    fwd_hi, fwd_lo, bwd_hi, bwd_lo = [
        jnp.take(x, order, axis=0).reshape(n_freq * fdev * 2, NT) for x in bases(n_freq, fdev)
    ]
    onset_part = lax.dynamic_slice(onset, (me_freq * vc, me_rcv * own), (vc, own))
    back = window_traces(spec, onset_part, fwd_hi.T, fwd_lo.T, bwd_hi, bwd_lo).reshape(n_freq, fdev, 2, vc, own)

    back_full = jnp.zeros((fdev, 2, vdev, own), jnp.float32)
    for shift in range(n_freq):
        piece = back[shift]
        if shift:
            piece = shifted(piece, "freq", n_freq - shift, n_freq)
        src = (me_freq + shift) % n_freq
        back_full = lax.dynamic_update_slice_in_dim(back_full, piece, src * vc, axis=2)

    adjoint = None
    for shift in range(n_rcv):
        piece = back_full
        if shift:
            piece = shifted(back_full, "rcv", shift, n_rcv)
        term = adjoint_chunk(refl_parts, piece, (me_rcv - shift) % n_rcv)
        adjoint = term if adjoint is None else adjoint + term
    return initial + adjoint


def solution(mesh):
    return jax.shard_map(
        per_device,
        mesh=mesh,
        in_specs=(
            P("grp", "freq", None, "rcv"),
            P(("grp", "freq"), None, "sub", "rcv"),
            P(("grp", "freq"), None, "sub", "rcv"),
            P(("grp", "sub"), None),
        ),
        out_specs=P(("grp", "freq"), None, "sub", "rcv"),
        check_vma=False,
    )
```

```python
import math

import jax
import jax.numpy as jnp
import numpy as np
from jax import lax
from jax.experimental import pallas as pl
from jax.experimental.pallas import tpu as pltpu
from jax.sharding import PartitionSpec as P

NT = 512
BF16 = jnp.bfloat16


def split(x):
    high = x.astype(BF16)
    return high, (x - high.astype(jnp.float32)).astype(BF16)


HIGHEST = lax.Precision.HIGHEST


def dot3(lhs3, rhs):
    r_hi, r_lo = split(rhs)
    stacked = jnp.concatenate([r_hi, r_lo, r_hi], axis=0)
    return jnp.dot(lhs3, stacked, preferred_element_type=jnp.float32)


def bases(n_freq_dev, fdev):
    bins = np.arange(1, n_freq_dev * fdev + 1, dtype=np.int64)
    samples = np.arange(NT, dtype=np.int64)
    phase = (bins[:, None] * samples[None, :] % NT).astype(np.float64) * (2.0 * math.pi / NT)
    cosine, sine = np.cos(phase), np.sin(phase)
    pair = np.stack([cosine, -sine], axis=1).reshape(n_freq_dev, fdev * 2, NT)
    fwd = ((2.0 / NT) * pair).astype(np.float32)
    bwd = pair.astype(np.float32)
    return [jnp.asarray(x) for x in split_np(fwd) + split_np(bwd)]


def split_np(x):
    high = x.astype(BF16)
    return [high, (x - high.astype(np.float32)).astype(BF16)]


def triple(high, low, axis):
    return jnp.concatenate([high, high, low], axis=axis)


def window_kernel(x_ref, onset_ref, fwd_ref, bwd_ref, out_ref):
    fwd = fwd_ref[...]
    bwd = bwd_ref[...]
    for v in range(x_ref.shape[1]):
        trace = dot3(fwd, x_ref[:, v, :])
        samples = lax.broadcasted_iota(jnp.int32, trace.shape, 0)
        windowed = jnp.where(samples < onset_ref[pl.ds(v, 1), :], trace, jnp.float32(0.0))
        out_ref[:, v, :] = dot3(bwd, windowed)


def window_traces(spec, onset_part, fwd3, bwd3):
    k2, nv, ns = spec.shape
    vt = 8 if nv % 8 == 0 else nv
    return pl.pallas_call(
        window_kernel,
        out_shape=jax.ShapeDtypeStruct((k2, nv, ns), jnp.float32),
        grid=(nv // vt,),
        in_specs=[
            pl.BlockSpec((k2, vt, ns), lambda i: (0, i, 0)),
            pl.BlockSpec((vt, ns), lambda i: (i, 0)),
            pl.BlockSpec((NT, 3 * k2), lambda i: (0, 0)),
            pl.BlockSpec((k2, 3 * NT), lambda i: (0, 0)),
        ],
        out_specs=pl.BlockSpec((k2, vt, ns), lambda i: (0, i, 0)),
        cost_estimate=pl.CostEstimate(
            flops=4 * NT * k2 * nv * ns * 3, transcendentals=0, bytes_accessed=(2 * k2 + 1) * nv * ns * 4
        ),
    )(spec, onset_part, fwd3, bwd3)


def product_chunk(reflection, focus_stack, chunk, size):
    vdev = focus_stack.shape[1] // 2
    refl = lax.dynamic_slice_in_dim(reflection, chunk * size, size, axis=2)
    ab = jnp.einsum("fwr,cfsr->fcws", focus_stack, refl, precision=HIGHEST)
    a, b = ab[:, 0], ab[:, 1]
    real = a[:, :vdev] - b[:, vdev:]
    imag = a[:, vdev:] + b[:, :vdev]
    return jnp.stack([real, imag], axis=1)


def adjoint_chunk(reflection, back, chunk):
    fdev, _, vdev, size = back.shape
    stacked = back.reshape(fdev, 2 * vdev, size)
    refl = lax.dynamic_slice_in_dim(reflection, chunk * size, size, axis=2)
    g = jnp.einsum("fws,cfsr->fcwr", stacked, refl, precision=HIGHEST)
    g_r, g_i = g[:, 0], g[:, 1]
    real = g_r[:, :vdev] + g_i[:, vdev:]
    imag = g_r[:, vdev:] - g_i[:, :vdev]
    return jnp.stack([real, imag], axis=1)


def shifted(x, axis, shift, n):
    return lax.ppermute(x, axis, [(i, (i + shift) % n) for i in range(n)])


def per_device(reflection, focus, initial, onset):
    _, fdev, total_src, nrcv_local = reflection.shape
    vdev = focus.shape[2]
    focus_stack = focus.reshape(fdev, 2 * vdev, nrcv_local)
    n_rcv = lax.axis_size("rcv")
    n_freq = lax.axis_size("freq")
    me_rcv = lax.axis_index("rcv")
    me_freq = lax.axis_index("freq")
    own = total_src // n_rcv
    vc = vdev // n_freq

    summed = None
    for shift in range(n_rcv):
        part = product_chunk(reflection, focus_stack, (me_rcv + shift) % n_rcv, own)
        if shift:
            part = shifted(part, "rcv", shift, n_rcv)
        summed = part if summed is None else summed + part

    blocks = []
    for shift in range(n_freq):
        dest = (me_freq + shift) % n_freq
        block = lax.dynamic_slice_in_dim(summed, dest * vc, vc, axis=2)
        if shift:
            block = shifted(block, "freq", shift, n_freq)
        blocks.append(block)
    spec = jnp.stack(blocks, axis=0).reshape(n_freq * fdev * 2, vc, own)
    order = (me_freq - jnp.arange(n_freq)) % n_freq
    fwd_hi, fwd_lo, bwd_hi, bwd_lo = [
        jnp.take(x, order, axis=0).reshape(n_freq * fdev * 2, NT) for x in bases(n_freq, fdev)
    ]
    onset_part = lax.dynamic_slice(onset, (me_freq * vc, me_rcv * own), (vc, own))
    fwd3 = triple(fwd_hi.T, fwd_lo.T, axis=1)
    bwd3 = triple(bwd_hi, bwd_lo, axis=1)
    back = window_traces(spec, onset_part, fwd3, bwd3).reshape(n_freq, fdev, 2, vc, own)

    back_full = jnp.zeros((fdev, 2, vdev, own), jnp.float32)
    for shift in range(n_freq):
        piece = back[shift]
        if shift:
            piece = shifted(piece, "freq", n_freq - shift, n_freq)
        src = (me_freq + shift) % n_freq
        back_full = lax.dynamic_update_slice_in_dim(back_full, piece, src * vc, axis=2)

    adjoint = None
    for shift in range(n_rcv):
        piece = back_full
        if shift:
            piece = shifted(back_full, "rcv", shift, n_rcv)
        term = adjoint_chunk(reflection, piece, (me_rcv - shift) % n_rcv)
        adjoint = term if adjoint is None else adjoint + term
    return initial + adjoint


def solution(mesh):
    return jax.shard_map(
        per_device,
        mesh=mesh,
        in_specs=(
            P("grp", "freq", None, "rcv"),
            P(("grp", "freq"), None, "sub", "rcv"),
            P(("grp", "freq"), None, "sub", "rcv"),
            P(("grp", "sub"), None),
        ),
        out_specs=P(("grp", "freq"), None, "sub", "rcv"),
        check_vma=False,
    )
```

```python
import math

import jax
import jax.numpy as jnp
import numpy as np
from jax import lax
from jax.experimental import pallas as pl
from jax.experimental.pallas import tpu as pltpu
from jax.sharding import PartitionSpec as P

NT = 512
BF16 = jnp.bfloat16


def split(x):
    high = x.astype(BF16)
    return high, (x - high.astype(jnp.float32)).astype(BF16)


HIGHEST = lax.Precision.HIGHEST


def dot3(lhs3, rhs):
    r_hi, r_lo = split(rhs)
    stacked = jnp.concatenate([r_hi, r_lo, r_hi], axis=0)
    return jnp.dot(lhs3, stacked, preferred_element_type=jnp.float32)


def bases(n_freq_dev, fdev):
    bins = np.arange(1, n_freq_dev * fdev + 1, dtype=np.int64)
    samples = np.arange(NT, dtype=np.int64)
    phase = (bins[:, None] * samples[None, :] % NT).astype(np.float64) * (2.0 * math.pi / NT)
    cosine, sine = np.cos(phase), np.sin(phase)
    pair = np.stack([cosine, -sine], axis=1).reshape(n_freq_dev, fdev * 2, NT)
    fwd = ((2.0 / NT) * pair).astype(np.float32)
    bwd = pair.astype(np.float32)
    return [jnp.asarray(x) for x in split_np(fwd) + split_np(bwd)]


def split_np(x):
    high = x.astype(BF16)
    return [high, (x - high.astype(np.float32)).astype(BF16)]


def triple(high, low, axis):
    return jnp.concatenate([high, high, low], axis=axis)


def window_kernel(x_ref, onset_ref, fwd_ref, bwd_ref, out_ref):
    fwd = fwd_ref[...]
    bwd = bwd_ref[...]
    for v in range(x_ref.shape[1]):
        trace = dot3(fwd, x_ref[:, v, :])
        samples = lax.broadcasted_iota(jnp.int32, trace.shape, 0)
        windowed = jnp.where(samples < onset_ref[pl.ds(v, 1), :], trace, jnp.float32(0.0))
        out_ref[:, v, :] = dot3(bwd, windowed)


def window_traces(spec, onset_part, fwd3, bwd3):
    k2, nv, ns = spec.shape
    vt = 8 if nv % 8 == 0 else nv
    return pl.pallas_call(
        window_kernel,
        out_shape=jax.ShapeDtypeStruct((k2, nv, ns), jnp.float32),
        grid=(nv // vt,),
        in_specs=[
            pl.BlockSpec((k2, vt, ns), lambda i: (0, i, 0)),
            pl.BlockSpec((vt, ns), lambda i: (i, 0)),
            pl.BlockSpec((NT, 3 * k2), lambda i: (0, 0)),
            pl.BlockSpec((k2, 3 * NT), lambda i: (0, 0)),
        ],
        out_specs=pl.BlockSpec((k2, vt, ns), lambda i: (0, i, 0)),
        cost_estimate=pl.CostEstimate(
            flops=4 * NT * k2 * nv * ns * 3, transcendentals=0, bytes_accessed=(2 * k2 + 1) * nv * ns * 4
        ),
    )(spec, onset_part, fwd3, bwd3)


def product_chunk(reflection, focus_stack, chunk, size):
    vdev = focus_stack.shape[1] // 2
    refl = lax.dynamic_slice_in_dim(reflection, chunk * size, size, axis=2)
    ab = jnp.einsum("fwr,cfsr->fcws", focus_stack, refl, precision=HIGHEST)
    a, b = ab[:, 0], ab[:, 1]
    real = a[:, :vdev] - b[:, vdev:]
    imag = a[:, vdev:] + b[:, :vdev]
    return jnp.stack([real, imag], axis=1)


def adjoint_chunk(reflection, back, chunk):
    fdev, _, vdev, size = back.shape
    stacked = back.reshape(fdev, 2 * vdev, size)
    refl = lax.dynamic_slice_in_dim(reflection, chunk * size, size, axis=2)
    g = jnp.einsum("fws,cfsr->fcwr", stacked, refl, precision=HIGHEST)
    g_r, g_i = g[:, 0], g[:, 1]
    real = g_r[:, :vdev] + g_i[:, vdev:]
    imag = g_r[:, vdev:] - g_i[:, :vdev]
    return jnp.stack([real, imag], axis=1)


def shifted(x, axis, shift, n):
    return lax.ppermute(x, axis, [(i, (i + shift) % n) for i in range(n)])


def pipeline(reflection, focus_stack, onset, v0):
    _, fdev, total_src, _ = reflection.shape
    vdev = focus_stack.shape[1] // 2
    n_rcv = lax.axis_size("rcv")
    n_freq = lax.axis_size("freq")
    me_rcv = lax.axis_index("rcv")
    me_freq = lax.axis_index("freq")
    own = total_src // n_rcv
    vc = vdev // n_freq

    summed = None
    for shift in range(n_rcv):
        part = product_chunk(reflection, focus_stack, (me_rcv + shift) % n_rcv, own)
        if shift:
            part = shifted(part, "rcv", shift, n_rcv)
        summed = part if summed is None else summed + part

    blocks = []
    for shift in range(n_freq):
        dest = (me_freq + shift) % n_freq
        block = lax.dynamic_slice_in_dim(summed, dest * vc, vc, axis=2)
        if shift:
            block = shifted(block, "freq", shift, n_freq)
        blocks.append(block)
    spec = jnp.stack(blocks, axis=0).reshape(n_freq * fdev * 2, vc, own)
    order = (me_freq - jnp.arange(n_freq)) % n_freq
    fwd_hi, fwd_lo, bwd_hi, bwd_lo = [
        jnp.take(x, order, axis=0).reshape(n_freq * fdev * 2, NT) for x in bases(n_freq, fdev)
    ]
    onset_part = lax.dynamic_slice(onset, (v0 + me_freq * vc, me_rcv * own), (vc, own))
    fwd3 = triple(fwd_hi.T, fwd_lo.T, axis=1)
    bwd3 = triple(bwd_hi, bwd_lo, axis=1)
    back = window_traces(spec, onset_part, fwd3, bwd3).reshape(n_freq, fdev, 2, vc, own)

    back_full = jnp.zeros((fdev, 2, vdev, own), jnp.float32)
    for shift in range(n_freq):
        piece = back[shift]
        if shift:
            piece = shifted(piece, "freq", n_freq - shift, n_freq)
        src = (me_freq + shift) % n_freq
        back_full = lax.dynamic_update_slice_in_dim(back_full, piece, src * vc, axis=2)

    adjoint = None
    for shift in range(n_rcv):
        piece = back_full
        if shift:
            piece = shifted(back_full, "rcv", shift, n_rcv)
        term = adjoint_chunk(reflection, piece, (me_rcv - shift) % n_rcv)
        adjoint = term if adjoint is None else adjoint + term
    return adjoint


def per_device(reflection, focus, initial, onset):
    fdev, _, vdev, nrcv_local = focus.shape
    n_freq = lax.axis_size("freq")
    halves = 2 if (vdev // 2) % n_freq == 0 else 1
    width = vdev // halves
    parts = []
    for h in range(halves):
        focus_h = focus[:, :, h * width:(h + 1) * width].reshape(fdev, 2 * width, nrcv_local)
        parts.append(pipeline(reflection, focus_h, onset, h * width))
    return initial + jnp.concatenate(parts, axis=2)


def solution(mesh):
    return jax.shard_map(
        per_device,
        mesh=mesh,
        in_specs=(
            P("grp", "freq", None, "rcv"),
            P(("grp", "freq"), None, "sub", "rcv"),
            P(("grp", "freq"), None, "sub", "rcv"),
            P(("grp", "sub"), None),
        ),
        out_specs=P(("grp", "freq"), None, "sub", "rcv"),
        check_vma=False,
    )
```

```python
import math

import jax
import jax.numpy as jnp
import numpy as np
from jax import lax
from jax.experimental import pallas as pl
from jax.experimental.pallas import tpu as pltpu
from jax.sharding import PartitionSpec as P

NT = 512
BF16 = jnp.bfloat16


def split(x):
    high = x.astype(BF16)
    return high, (x - high.astype(jnp.float32)).astype(BF16)


HIGHEST = lax.Precision.HIGHEST


def dot3(lhs3, rhs):
    r_hi, r_lo = split(rhs)
    stacked = jnp.concatenate([r_hi, r_lo, r_hi], axis=0)
    return jnp.dot(lhs3, stacked, preferred_element_type=jnp.float32)


def bases(n_freq_dev, fdev):
    bins = np.arange(1, n_freq_dev * fdev + 1, dtype=np.int64)
    samples = np.arange(NT, dtype=np.int64)
    phase = (bins[:, None] * samples[None, :] % NT).astype(np.float64) * (2.0 * math.pi / NT)
    cosine, sine = np.cos(phase), np.sin(phase)
    pair = np.stack([cosine, -sine], axis=1).reshape(n_freq_dev * fdev * 2, NT)
    fwd_hi, fwd_lo = split_np(((2.0 / NT) * pair).astype(np.float32).T)
    bwd_hi, bwd_lo = split_np(pair.astype(np.float32))
    fwd3 = np.concatenate([fwd_hi, fwd_hi, fwd_lo], axis=1)
    bwd3 = np.concatenate([bwd_hi, bwd_hi, bwd_lo], axis=1)
    return jnp.asarray(fwd3), jnp.asarray(bwd3)


def split_np(x):
    high = x.astype(BF16)
    return [high, (x - high.astype(np.float32)).astype(BF16)]


def window_kernel(x_ref, onset_ref, fwd_ref, bwd_ref, out_ref):
    fwd = fwd_ref[...]
    bwd = bwd_ref[...]
    for v in range(x_ref.shape[1]):
        trace = dot3(fwd, x_ref[:, v, :])
        samples = lax.broadcasted_iota(jnp.int32, trace.shape, 0)
        windowed = jnp.where(samples < onset_ref[pl.ds(v, 1), :], trace, jnp.float32(0.0))
        out_ref[:, v, :] = dot3(bwd, windowed)


def window_traces(spec, onset_part, fwd3, bwd3):
    k2, nv, ns = spec.shape
    vt = 8 if nv % 8 == 0 else nv
    return pl.pallas_call(
        window_kernel,
        out_shape=jax.ShapeDtypeStruct((k2, nv, ns), jnp.float32),
        grid=(nv // vt,),
        in_specs=[
            pl.BlockSpec((k2, vt, ns), lambda i: (0, i, 0)),
            pl.BlockSpec((vt, ns), lambda i: (i, 0)),
            pl.BlockSpec((NT, 3 * k2), lambda i: (0, 0)),
            pl.BlockSpec((k2, 3 * NT), lambda i: (0, 0)),
        ],
        out_specs=pl.BlockSpec((k2, vt, ns), lambda i: (0, i, 0)),
        cost_estimate=pl.CostEstimate(
            flops=4 * NT * k2 * nv * ns * 3, transcendentals=0, bytes_accessed=(2 * k2 + 1) * nv * ns * 4
        ),
    )(spec, onset_part, fwd3, bwd3)


def product_chunk(reflection, focus_stack, chunk, size):
    vdev = focus_stack.shape[1] // 2
    refl = lax.dynamic_slice_in_dim(reflection, chunk * size, size, axis=2)
    ab = jnp.einsum("fwr,cfsr->fcws", focus_stack, refl, precision=HIGHEST)
    a, b = ab[:, 0], ab[:, 1]
    real = a[:, :vdev] - b[:, vdev:]
    imag = a[:, vdev:] + b[:, :vdev]
    return jnp.stack([real, imag], axis=1)


def adjoint_chunk(reflection, back, chunk):
    fdev, _, vdev, size = back.shape
    stacked = back.reshape(fdev, 2 * vdev, size)
    refl = lax.dynamic_slice_in_dim(reflection, chunk * size, size, axis=2)
    g = jnp.einsum("fws,cfsr->fcwr", stacked, refl, precision=HIGHEST)
    g_r, g_i = g[:, 0], g[:, 1]
    real = g_r[:, :vdev] + g_i[:, vdev:]
    imag = g_r[:, vdev:] - g_i[:, :vdev]
    return jnp.stack([real, imag], axis=1)


def shifted(x, axis, shift, n):
    return lax.ppermute(x, axis, [(i, (i + shift) % n) for i in range(n)])


def window_half(summed, reflection, onset, v0, width):
    fdev, _, _, own = summed.shape
    n_rcv = lax.axis_size("rcv")
    n_freq = lax.axis_size("freq")
    me_rcv = lax.axis_index("rcv")
    me_freq = lax.axis_index("freq")
    vc = width // n_freq

    spec = jnp.zeros((n_freq, fdev, 2, vc, own), jnp.float32)
    for shift in range(n_freq):
        dest = (me_freq + shift) % n_freq
        block = lax.dynamic_slice_in_dim(summed, v0 + dest * vc, vc, axis=2)
        if shift:
            block = shifted(block, "freq", shift, n_freq)
        src = (me_freq - shift) % n_freq
        spec = lax.dynamic_update_index_in_dim(spec, block, src, axis=0)
    fwd3, bwd3 = bases(n_freq, fdev)
    onset_part = lax.dynamic_slice(onset, (v0 + me_freq * vc, me_rcv * own), (vc, own))
    back = window_traces(spec.reshape(n_freq * fdev * 2, vc, own), onset_part, fwd3, bwd3)
    back = back.reshape(n_freq, fdev, 2, vc, own)

    back_full = jnp.zeros((fdev, 2, width, own), jnp.float32)
    for shift in range(n_freq):
        piece = lax.dynamic_index_in_dim(back, (me_freq + shift) % n_freq, axis=0, keepdims=False)
        if shift:
            piece = shifted(piece, "freq", shift, n_freq)
        src = (me_freq - shift) % n_freq
        back_full = lax.dynamic_update_slice_in_dim(back_full, piece, src * vc, axis=2)

    adjoint = None
    for shift in range(n_rcv):
        piece = back_full
        if shift:
            piece = shifted(back_full, "rcv", shift, n_rcv)
        term = adjoint_chunk(reflection, piece, (me_rcv - shift) % n_rcv)
        adjoint = term if adjoint is None else adjoint + term
    return adjoint


def per_device(reflection, focus, initial, onset):
    _, fdev, total_src, nrcv_local = reflection.shape
    vdev = focus.shape[2]
    focus_stack = focus.reshape(fdev, 2 * vdev, nrcv_local)
    n_rcv = lax.axis_size("rcv")
    n_freq = lax.axis_size("freq")
    me_rcv = lax.axis_index("rcv")
    own = total_src // n_rcv

    summed = None
    for shift in range(n_rcv):
        part = product_chunk(reflection, focus_stack, (me_rcv + shift) % n_rcv, own)
        if shift:
            part = shifted(part, "rcv", shift, n_rcv)
        summed = part if summed is None else summed + part

    halves = 2 if (vdev // 2) % n_freq == 0 else 1
    width = vdev // halves
    parts = [window_half(summed, reflection, onset, h * width, width) for h in range(halves)]
    return initial + jnp.concatenate(parts, axis=2)


def solution(mesh):
    return jax.shard_map(
        per_device,
        mesh=mesh,
        in_specs=(
            P("grp", "freq", None, "rcv"),
            P(("grp", "freq"), None, "sub", "rcv"),
            P(("grp", "freq"), None, "sub", "rcv"),
            P(("grp", "sub"), None),
        ),
        out_specs=P(("grp", "freq"), None, "sub", "rcv"),
        check_vma=False,
    )
```

```python
import math

import jax
import jax.numpy as jnp
import numpy as np
from jax import lax
from jax.experimental import pallas as pl
from jax.experimental.pallas import tpu as pltpu
from jax.sharding import PartitionSpec as P

NT = 512
BF16 = jnp.bfloat16


def split(x):
    high = x.astype(BF16)
    return high, (x - high.astype(jnp.float32)).astype(BF16)


HIGHEST = lax.Precision.HIGHEST


def dot3(lhs3, rhs):
    r_hi, r_lo = split(rhs)
    stacked = jnp.concatenate([r_hi, r_lo, r_hi], axis=0)
    return jnp.dot(lhs3, stacked, preferred_element_type=jnp.float32)


def bases(n_freq_dev, fdev):
    bins = np.arange(1, n_freq_dev * fdev + 1, dtype=np.int64)
    samples = np.arange(NT, dtype=np.int64)
    phase = (bins[:, None] * samples[None, :] % NT).astype(np.float64) * (2.0 * math.pi / NT)
    cosine, sine = np.cos(phase), np.sin(phase)
    pair = np.stack([cosine, -sine], axis=1).reshape(n_freq_dev * fdev * 2, NT)
    fwd_hi, fwd_lo = split_np(((2.0 / NT) * pair).astype(np.float32).T)
    bwd_hi, bwd_lo = split_np(pair.astype(np.float32))
    fwd3 = np.concatenate([fwd_hi, fwd_hi, fwd_lo], axis=1)
    bwd3 = np.concatenate([bwd_hi, bwd_hi, bwd_lo], axis=1)
    return jnp.asarray(fwd3), jnp.asarray(bwd3)


def split_np(x):
    high = x.astype(BF16)
    return [high, (x - high.astype(np.float32)).astype(BF16)]


def window_kernel(x_ref, onset_ref, fwd_ref, bwd_ref, out_ref):
    fwd = fwd_ref[...]
    bwd = bwd_ref[...]
    for v in range(x_ref.shape[1]):
        trace = dot3(fwd, x_ref[:, v, :])
        samples = lax.broadcasted_iota(jnp.int32, trace.shape, 0)
        windowed = jnp.where(samples < onset_ref[pl.ds(v, 1), :], trace, jnp.float32(0.0))
        out_ref[:, v, :] = dot3(bwd, windowed)


def window_traces(spec, onset_part, fwd3, bwd3):
    k2, nv, ns = spec.shape
    vt = 8 if nv % 8 == 0 else nv
    return pl.pallas_call(
        window_kernel,
        out_shape=jax.ShapeDtypeStruct((k2, nv, ns), jnp.float32),
        grid=(nv // vt,),
        in_specs=[
            pl.BlockSpec((k2, vt, ns), lambda i: (0, i, 0)),
            pl.BlockSpec((vt, ns), lambda i: (i, 0)),
            pl.BlockSpec((NT, 3 * k2), lambda i: (0, 0)),
            pl.BlockSpec((k2, 3 * NT), lambda i: (0, 0)),
        ],
        out_specs=pl.BlockSpec((k2, vt, ns), lambda i: (0, i, 0)),
        cost_estimate=pl.CostEstimate(
            flops=4 * NT * k2 * nv * ns * 3, transcendentals=0, bytes_accessed=(2 * k2 + 1) * nv * ns * 4
        ),
    )(spec, onset_part, fwd3, bwd3)


def product_kernel(chunk_ref, focus_ref, refl_ref, out_ref):
    vdev = focus_ref.shape[1] // 2
    f_hi, f_lo = split(focus_ref[0])
    lhs = jnp.concatenate([f_hi, f_hi, f_lo], axis=1)
    terms = []
    for part in range(2):
        r_hi, r_lo = split(refl_ref[part, 0])
        rhs = jnp.concatenate([r_hi, r_lo, r_hi], axis=1)
        terms.append(lax.dot_general(lhs, rhs, (((1,), (1,)), ((), ())), preferred_element_type=jnp.float32))
    a, b = terms
    out_ref[0, 0] = a[:vdev] - b[vdev:]
    out_ref[0, 1] = a[vdev:] + b[:vdev]


def product_chunk(reflection, focus_stack, chunk, size):
    _, fdev, _, nr = reflection.shape
    w2 = focus_stack.shape[1]
    return pl.pallas_call(
        product_kernel,
        out_shape=jax.ShapeDtypeStruct((fdev, 2, w2 // 2, size), jnp.float32),
        grid_spec=pltpu.PrefetchScalarGridSpec(
            num_scalar_prefetch=1,
            grid=(fdev,),
            in_specs=[
                pl.BlockSpec((1, w2, nr), lambda f, c: (f, 0, 0)),
                pl.BlockSpec((2, 1, size, nr), lambda f, c: (0, f, c[0], 0)),
            ],
            out_specs=pl.BlockSpec((1, 2, w2 // 2, size), lambda f, c: (f, 0, 0, 0)),
        ),
        cost_estimate=pl.CostEstimate(
            flops=2 * 2 * fdev * w2 * size * nr * 3, transcendentals=0, bytes_accessed=4 * fdev * (2 * size + w2) * nr
        ),
    )(jnp.reshape(chunk, (1,)).astype(jnp.int32), focus_stack, reflection)


def adjoint_kernel(chunk_ref, back_ref, refl_ref, out_ref):
    width = back_ref.shape[2]
    b_hi, b_lo = split(back_ref[0].reshape(2 * width, back_ref.shape[3]))
    lhs = jnp.concatenate([b_hi, b_hi, b_lo], axis=1)
    terms = []
    for part in range(2):
        r_hi, r_lo = split(refl_ref[part, 0])
        rhs = jnp.concatenate([r_hi, r_lo, r_hi], axis=0)
        terms.append(jnp.dot(lhs, rhs, preferred_element_type=jnp.float32))
    g_r, g_i = terms
    out_ref[0, 0] = g_r[:width] + g_i[width:]
    out_ref[0, 1] = g_r[width:] - g_i[:width]


def adjoint_chunk(reflection, back, chunk):
    _, fdev, _, nr = reflection.shape
    _, _, width, size = back.shape
    return pl.pallas_call(
        adjoint_kernel,
        out_shape=jax.ShapeDtypeStruct((fdev, 2, width, nr), jnp.float32),
        grid_spec=pltpu.PrefetchScalarGridSpec(
            num_scalar_prefetch=1,
            grid=(fdev,),
            in_specs=[
                pl.BlockSpec((1, 2, width, size), lambda f, c: (f, 0, 0, 0)),
                pl.BlockSpec((2, 1, size, nr), lambda f, c: (0, f, c[0], 0)),
            ],
            out_specs=pl.BlockSpec((1, 2, width, nr), lambda f, c: (f, 0, 0, 0)),
        ),
        cost_estimate=pl.CostEstimate(
            flops=2 * 2 * fdev * 2 * width * size * nr * 3, transcendentals=0,
            bytes_accessed=4 * fdev * (2 * size * nr + 2 * width * (size + nr)),
        ),
    )(jnp.reshape(chunk, (1,)).astype(jnp.int32), back, reflection)


def shifted(x, axis, shift, n):
    return lax.ppermute(x, axis, [(i, (i + shift) % n) for i in range(n)])


def window_half(summed, reflection, onset, v0, width):
    fdev, _, _, own = summed.shape
    n_rcv = lax.axis_size("rcv")
    n_freq = lax.axis_size("freq")
    me_rcv = lax.axis_index("rcv")
    me_freq = lax.axis_index("freq")
    vc = width // n_freq

    spec = jnp.zeros((n_freq, fdev, 2, vc, own), jnp.float32)
    for shift in range(n_freq):
        dest = (me_freq + shift) % n_freq
        block = lax.dynamic_slice_in_dim(summed, v0 + dest * vc, vc, axis=2)
        if shift:
            block = shifted(block, "freq", shift, n_freq)
        src = (me_freq - shift) % n_freq
        spec = lax.dynamic_update_index_in_dim(spec, block, src, axis=0)
    fwd3, bwd3 = bases(n_freq, fdev)
    onset_part = lax.dynamic_slice(onset, (v0 + me_freq * vc, me_rcv * own), (vc, own))
    back = window_traces(spec.reshape(n_freq * fdev * 2, vc, own), onset_part, fwd3, bwd3)
    back = back.reshape(n_freq, fdev, 2, vc, own)

    back_full = jnp.zeros((fdev, 2, width, own), jnp.float32)
    for shift in range(n_freq):
        piece = lax.dynamic_index_in_dim(back, (me_freq + shift) % n_freq, axis=0, keepdims=False)
        if shift:
            piece = shifted(piece, "freq", shift, n_freq)
        src = (me_freq - shift) % n_freq
        back_full = lax.dynamic_update_slice_in_dim(back_full, piece, src * vc, axis=2)

    adjoint = None
    for shift in range(n_rcv):
        piece = back_full
        if shift:
            piece = shifted(back_full, "rcv", shift, n_rcv)
        term = adjoint_chunk(reflection, piece, (me_rcv - shift) % n_rcv)
        adjoint = term if adjoint is None else adjoint + term
    return adjoint


def per_device(reflection, focus, initial, onset):
    _, fdev, total_src, nrcv_local = reflection.shape
    vdev = focus.shape[2]
    focus_stack = focus.reshape(fdev, 2 * vdev, nrcv_local)
    n_rcv = lax.axis_size("rcv")
    n_freq = lax.axis_size("freq")
    me_rcv = lax.axis_index("rcv")
    own = total_src // n_rcv

    summed = None
    for shift in range(n_rcv):
        part = product_chunk(reflection, focus_stack, (me_rcv + shift) % n_rcv, own)
        if shift:
            part = shifted(part, "rcv", shift, n_rcv)
        summed = part if summed is None else summed + part

    halves = 2 if (vdev // 2) % n_freq == 0 else 1
    width = vdev // halves
    parts = [window_half(summed, reflection, onset, h * width, width) for h in range(halves)]
    return initial + jnp.concatenate(parts, axis=2)


def solution(mesh):
    return jax.shard_map(
        per_device,
        mesh=mesh,
        in_specs=(
            P("grp", "freq", None, "rcv"),
            P(("grp", "freq"), None, "sub", "rcv"),
            P(("grp", "freq"), None, "sub", "rcv"),
            P(("grp", "sub"), None),
        ),
        out_specs=P(("grp", "freq"), None, "sub", "rcv"),
        check_vma=False,
    )
```

```python
import math

import jax
import jax.numpy as jnp
import numpy as np
from jax import lax
from jax.experimental import pallas as pl
from jax.experimental.pallas import tpu as pltpu
from jax.sharding import PartitionSpec as P

NT = 512
BF16 = jnp.bfloat16


def split(x):
    high = x.astype(BF16)
    return high, (x - high.astype(jnp.float32)).astype(BF16)


HIGHEST = lax.Precision.HIGHEST


def dot3(lhs3, rhs):
    r_hi, r_lo = split(rhs)
    stacked = jnp.concatenate([r_hi, r_lo, r_hi], axis=0)
    return jnp.dot(lhs3, stacked, preferred_element_type=jnp.float32)


def bases(n_freq_dev, fdev):
    bins = np.arange(1, n_freq_dev * fdev + 1, dtype=np.int64)
    samples = np.arange(NT, dtype=np.int64)
    phase = (bins[:, None] * samples[None, :] % NT).astype(np.float64) * (2.0 * math.pi / NT)
    cosine, sine = np.cos(phase), np.sin(phase)
    pair = np.stack([cosine, -sine], axis=1).reshape(n_freq_dev * fdev * 2, NT)
    fwd_hi, fwd_lo = split_np(((2.0 / NT) * pair).astype(np.float32).T)
    bwd_hi, bwd_lo = split_np(pair.astype(np.float32))
    fwd3 = np.concatenate([fwd_hi, fwd_hi, fwd_lo], axis=1)
    bwd3 = np.concatenate([bwd_hi, bwd_hi, bwd_lo], axis=1)
    return jnp.asarray(fwd3), jnp.asarray(bwd3)


def split_np(x):
    high = x.astype(BF16)
    return [high, (x - high.astype(np.float32)).astype(BF16)]


def window_kernel(x_ref, onset_ref, fwd_ref, bwd_ref, out_ref):
    fwd = fwd_ref[...]
    bwd = bwd_ref[...]
    for v in range(x_ref.shape[1]):
        trace = dot3(fwd, x_ref[:, v, :])
        samples = lax.broadcasted_iota(jnp.int32, trace.shape, 0)
        windowed = jnp.where(samples < onset_ref[pl.ds(v, 1), :], trace, jnp.float32(0.0))
        out_ref[:, v, :] = dot3(bwd, windowed)


def window_traces(spec, onset_part, fwd3, bwd3):
    k2, nv, ns = spec.shape
    vt = 8 if nv % 8 == 0 else nv
    return pl.pallas_call(
        window_kernel,
        out_shape=jax.ShapeDtypeStruct((k2, nv, ns), jnp.float32),
        grid=(nv // vt,),
        in_specs=[
            pl.BlockSpec((k2, vt, ns), lambda i: (0, i, 0)),
            pl.BlockSpec((vt, ns), lambda i: (i, 0)),
            pl.BlockSpec((NT, 3 * k2), lambda i: (0, 0)),
            pl.BlockSpec((k2, 3 * NT), lambda i: (0, 0)),
        ],
        out_specs=pl.BlockSpec((k2, vt, ns), lambda i: (0, i, 0)),
        cost_estimate=pl.CostEstimate(
            flops=4 * NT * k2 * nv * ns * 3, transcendentals=0, bytes_accessed=(2 * k2 + 1) * nv * ns * 4
        ),
    )(spec, onset_part, fwd3, bwd3)


def product_chunk(reflection, focus_stack, chunk, size):
    vdev = focus_stack.shape[1] // 2
    refl = lax.dynamic_slice_in_dim(reflection, chunk * size, size, axis=2)
    ab = jnp.einsum("fwr,cfsr->fcws", focus_stack, refl, precision=HIGHEST)
    a, b = ab[:, 0], ab[:, 1]
    real = a[:, :vdev] - b[:, vdev:]
    imag = a[:, vdev:] + b[:, :vdev]
    return jnp.stack([real, imag], axis=1)


def adjoint_chunk(reflection, back, chunk):
    fdev, _, vdev, size = back.shape
    stacked = back.reshape(fdev, 2 * vdev, size)
    refl = lax.dynamic_slice_in_dim(reflection, chunk * size, size, axis=2)
    g = jnp.einsum("fws,cfsr->fcwr", stacked, refl, precision=HIGHEST)
    g_r, g_i = g[:, 0], g[:, 1]
    real = g_r[:, :vdev] + g_i[:, vdev:]
    imag = g_r[:, vdev:] - g_i[:, :vdev]
    return jnp.stack([real, imag], axis=1)


def shifted(x, axis, shift, n):
    return lax.ppermute(x, axis, [(i, (i + shift) % n) for i in range(n)])


def window_half(summed, reflection, onset, v0):
    fdev, _, width, own = summed.shape
    n_rcv = lax.axis_size("rcv")
    n_freq = lax.axis_size("freq")
    me_rcv = lax.axis_index("rcv")
    me_freq = lax.axis_index("freq")
    vc = width // n_freq

    spec = jnp.zeros((n_freq, fdev, 2, vc, own), jnp.float32)
    for shift in range(n_freq):
        dest = (me_freq + shift) % n_freq
        block = lax.dynamic_slice_in_dim(summed, dest * vc, vc, axis=2)
        if shift:
            block = shifted(block, "freq", shift, n_freq)
        src = (me_freq - shift) % n_freq
        spec = lax.dynamic_update_index_in_dim(spec, block, src, axis=0)
    fwd3, bwd3 = bases(n_freq, fdev)
    onset_part = lax.dynamic_slice(onset, (v0 + me_freq * vc, me_rcv * own), (vc, own))
    back = window_traces(spec.reshape(n_freq * fdev * 2, vc, own), onset_part, fwd3, bwd3)
    back = back.reshape(n_freq, fdev, 2, vc, own)

    back_full = jnp.zeros((fdev, 2, width, own), jnp.float32)
    for shift in range(n_freq):
        piece = lax.dynamic_index_in_dim(back, (me_freq + shift) % n_freq, axis=0, keepdims=False)
        if shift:
            piece = shifted(piece, "freq", shift, n_freq)
        src = (me_freq - shift) % n_freq
        back_full = lax.dynamic_update_slice_in_dim(back_full, piece, src * vc, axis=2)

    adjoint = None
    for shift in range(n_rcv):
        piece = back_full
        if shift:
            piece = shifted(back_full, "rcv", shift, n_rcv)
        term = adjoint_chunk(reflection, piece, (me_rcv - shift) % n_rcv)
        adjoint = term if adjoint is None else adjoint + term
    return adjoint


def per_device(reflection, focus, initial, onset):
    _, fdev, total_src, nrcv_local = reflection.shape
    vdev = focus.shape[2]
    focus_stack = focus.reshape(fdev, 2 * vdev, nrcv_local)
    n_rcv = lax.axis_size("rcv")
    n_freq = lax.axis_size("freq")
    me_rcv = lax.axis_index("rcv")
    own = total_src // n_rcv

    halves = 2 if (vdev // 2) % n_freq == 0 else 1
    width = vdev // halves

    summed = [None] * halves
    for shift in range(n_rcv):
        part = product_chunk(reflection, focus_stack, (me_rcv + shift) % n_rcv, own)
        for h in range(halves):
            piece = part[:, :, h * width:(h + 1) * width]
            if shift:
                piece = shifted(piece, "rcv", shift, n_rcv)
            summed[h] = piece if summed[h] is None else summed[h] + piece
    parts = [window_half(summed[h], reflection, onset, h * width) for h in range(halves)]
    return initial + jnp.concatenate(parts, axis=2)


def solution(mesh):
    return jax.shard_map(
        per_device,
        mesh=mesh,
        in_specs=(
            P("grp", "freq", None, "rcv"),
            P(("grp", "freq"), None, "sub", "rcv"),
            P(("grp", "freq"), None, "sub", "rcv"),
            P(("grp", "sub"), None),
        ),
        out_specs=P(("grp", "freq"), None, "sub", "rcv"),
        check_vma=False,
    )
```

```python
import math

import jax
import jax.numpy as jnp
import numpy as np
from jax import lax
from jax.experimental import pallas as pl
from jax.experimental.pallas import tpu as pltpu
from jax.sharding import PartitionSpec as P

NT = 512
BF16 = jnp.bfloat16


def split(x):
    high = x.astype(BF16)
    return high, (x - high.astype(jnp.float32)).astype(BF16)


HIGHEST = lax.Precision.HIGHEST


def dot3(lhs3, rhs):
    r_hi, r_lo = split(rhs)
    stacked = jnp.concatenate([r_hi, r_lo, r_hi], axis=0)
    return jnp.dot(lhs3, stacked, preferred_element_type=jnp.float32)


def bases(n_freq_dev, fdev):
    bins = np.arange(1, n_freq_dev * fdev + 1, dtype=np.int64)
    samples = np.arange(NT, dtype=np.int64)
    phase = (bins[:, None] * samples[None, :] % NT).astype(np.float64) * (2.0 * math.pi / NT)
    cosine, sine = np.cos(phase), np.sin(phase)
    pair = np.stack([cosine, -sine], axis=1).reshape(n_freq_dev * fdev * 2, NT)
    fwd_hi, fwd_lo = split_np(((2.0 / NT) * pair).astype(np.float32).T)
    bwd_hi, bwd_lo = split_np(pair.astype(np.float32))
    fwd3 = np.concatenate([fwd_hi, fwd_hi, fwd_lo], axis=1)
    bwd3 = np.concatenate([bwd_hi, bwd_hi, bwd_lo], axis=1)
    return jnp.asarray(fwd3), jnp.asarray(bwd3)


def split_np(x):
    high = x.astype(BF16)
    return [high, (x - high.astype(np.float32)).astype(BF16)]


def window_kernel(x_ref, onset_ref, fwd_ref, bwd_ref, out_ref):
    fwd = fwd_ref[...]
    bwd = bwd_ref[...]
    for v in range(x_ref.shape[1]):
        trace = dot3(fwd, x_ref[:, v, :])
        samples = lax.broadcasted_iota(jnp.int32, trace.shape, 0)
        windowed = jnp.where(samples < onset_ref[pl.ds(v, 1), :], trace, jnp.float32(0.0))
        out_ref[:, v, :] = dot3(bwd, windowed)


def window_traces(spec, onset_part, fwd3, bwd3):
    k2, nv, ns = spec.shape
    vt = 8 if nv % 8 == 0 else nv
    return pl.pallas_call(
        window_kernel,
        out_shape=jax.ShapeDtypeStruct((k2, nv, ns), jnp.float32),
        grid=(nv // vt,),
        in_specs=[
            pl.BlockSpec((k2, vt, ns), lambda i: (0, i, 0)),
            pl.BlockSpec((vt, ns), lambda i: (i, 0)),
            pl.BlockSpec((NT, 3 * k2), lambda i: (0, 0)),
            pl.BlockSpec((k2, 3 * NT), lambda i: (0, 0)),
        ],
        out_specs=pl.BlockSpec((k2, vt, ns), lambda i: (0, i, 0)),
        cost_estimate=pl.CostEstimate(
            flops=4 * NT * k2 * nv * ns * 3, transcendentals=0, bytes_accessed=(2 * k2 + 1) * nv * ns * 4
        ),
    )(spec, onset_part, fwd3, bwd3)


def product_chunk(reflection, focus_stack, chunk, size):
    vdev = focus_stack.shape[1] // 2
    refl = lax.dynamic_slice_in_dim(reflection, chunk * size, size, axis=2)
    ab = jnp.einsum("fwr,cfsr->fcws", focus_stack, refl, precision=HIGHEST)
    a, b = ab[:, 0], ab[:, 1]
    real = a[:, :vdev] - b[:, vdev:]
    imag = a[:, vdev:] + b[:, :vdev]
    return jnp.stack([real, imag], axis=1)


def adjoint_chunk(reflection, back, chunk):
    fdev, _, vdev, size = back.shape
    stacked = back.reshape(fdev, 2 * vdev, size)
    refl = lax.dynamic_slice_in_dim(reflection, chunk * size, size, axis=2)
    g = jnp.einsum("fws,cfsr->fcwr", stacked, refl, precision=HIGHEST)
    g_r, g_i = g[:, 0], g[:, 1]
    real = g_r[:, :vdev] + g_i[:, vdev:]
    imag = g_r[:, vdev:] - g_i[:, :vdev]
    return jnp.stack([real, imag], axis=1)


def shifted(x, axis, shift, n):
    return lax.ppermute(x, axis, [(i, (i + shift) % n) for i in range(n)])


def window_half(summed, reflection, onset, v0):
    fdev, _, width, own = summed.shape
    n_rcv = lax.axis_size("rcv")
    n_freq = lax.axis_size("freq")
    me_rcv = lax.axis_index("rcv")
    me_freq = lax.axis_index("freq")
    vc = width // n_freq

    chunks = jnp.transpose(summed.reshape(fdev, 2, n_freq, vc, own), (2, 0, 1, 3, 4))
    spec = lax.all_to_all(chunks, "freq", 0, 0, tiled=True)
    fwd3, bwd3 = bases(n_freq, fdev)
    onset_part = lax.dynamic_slice(onset, (v0 + me_freq * vc, me_rcv * own), (vc, own))
    back = window_traces(spec.reshape(n_freq * fdev * 2, vc, own), onset_part, fwd3, bwd3)
    back = back.reshape(n_freq, fdev, 2, vc, own)

    back = lax.all_to_all(back, "freq", 0, 0, tiled=True)
    back_full = jnp.transpose(back, (1, 2, 0, 3, 4)).reshape(fdev, 2, width, own)

    adjoint = None
    for shift in range(n_rcv):
        piece = back_full
        if shift:
            piece = shifted(back_full, "rcv", shift, n_rcv)
        term = adjoint_chunk(reflection, piece, (me_rcv - shift) % n_rcv)
        adjoint = term if adjoint is None else adjoint + term
    return adjoint


def per_device(reflection, focus, initial, onset):
    _, fdev, total_src, nrcv_local = reflection.shape
    vdev = focus.shape[2]
    focus_stack = focus.reshape(fdev, 2 * vdev, nrcv_local)
    n_rcv = lax.axis_size("rcv")
    n_freq = lax.axis_size("freq")
    me_rcv = lax.axis_index("rcv")
    own = total_src // n_rcv

    halves = 2 if (vdev // 2) % n_freq == 0 else 1
    width = vdev // halves

    summed = [None] * halves
    for shift in range(n_rcv):
        part = product_chunk(reflection, focus_stack, (me_rcv + shift) % n_rcv, own)
        for h in range(halves):
            piece = part[:, :, h * width:(h + 1) * width]
            if shift:
                piece = shifted(piece, "rcv", shift, n_rcv)
            summed[h] = piece if summed[h] is None else summed[h] + piece
    parts = [window_half(summed[h], reflection, onset, h * width) for h in range(halves)]
    return initial + jnp.concatenate(parts, axis=2)


def solution(mesh):
    return jax.shard_map(
        per_device,
        mesh=mesh,
        in_specs=(
            P("grp", "freq", None, "rcv"),
            P(("grp", "freq"), None, "sub", "rcv"),
            P(("grp", "freq"), None, "sub", "rcv"),
            P(("grp", "sub"), None),
        ),
        out_specs=P(("grp", "freq"), None, "sub", "rcv"),
        check_vma=False,
    )
```

```python
import math

import jax
import jax.numpy as jnp
import numpy as np
from jax import lax
from jax.experimental import pallas as pl
from jax.experimental.pallas import tpu as pltpu
from jax.sharding import PartitionSpec as P

NT = 512
BF16 = jnp.bfloat16


def split(x):
    high = x.astype(BF16)
    return high, (x - high.astype(jnp.float32)).astype(BF16)


HIGHEST = lax.Precision.HIGHEST


def dot3(lhs3, rhs):
    r_hi, r_lo = split(rhs)
    stacked = jnp.concatenate([r_hi, r_lo, r_hi], axis=0)
    return jnp.dot(lhs3, stacked, preferred_element_type=jnp.float32)


def bases(n_freq_dev, fdev):
    bins = np.arange(1, n_freq_dev * fdev + 1, dtype=np.int64)
    samples = np.arange(NT, dtype=np.int64)
    phase = (bins[:, None] * samples[None, :] % NT).astype(np.float64) * (2.0 * math.pi / NT)
    cosine, sine = np.cos(phase), np.sin(phase)
    pair = np.stack([cosine, -sine], axis=1).reshape(n_freq_dev * fdev * 2, NT)
    fwd_hi, fwd_lo = split_np(((2.0 / NT) * pair).astype(np.float32).T)
    bwd_hi, bwd_lo = split_np(pair.astype(np.float32))
    fwd3 = np.concatenate([fwd_hi, fwd_hi, fwd_lo], axis=1)
    bwd2 = np.concatenate([bwd_hi, bwd_lo], axis=0)
    return jnp.asarray(fwd3), jnp.asarray(bwd2)


def split_np(x):
    high = x.astype(BF16)
    return [high, (x - high.astype(np.float32)).astype(BF16)]


def window_kernel(x_ref, onset_ref, fwd_ref, bwd_ref, out_ref):
    k2 = x_ref.shape[0]
    fwd = fwd_ref[...]
    bwd = bwd_ref[...]
    bwd_hi = bwd_ref[:k2, :]
    for v in range(x_ref.shape[1]):
        trace = dot3(fwd, x_ref[:, v, :])
        samples = lax.broadcasted_iota(jnp.int32, trace.shape, 0)
        windowed = jnp.where(samples < onset_ref[pl.ds(v, 1), :], trace, jnp.float32(0.0))
        w_hi, w_lo = split(windowed)
        both = jnp.dot(bwd, w_hi, preferred_element_type=jnp.float32)
        cross = jnp.dot(bwd_hi, w_lo, preferred_element_type=jnp.float32)
        out_ref[:, v, :] = both[:k2] + (both[k2:] + cross)


def window_traces(spec, onset_part, fwd3, bwd2):
    k2, nv, ns = spec.shape
    vt = 8 if nv % 8 == 0 else nv
    return pl.pallas_call(
        window_kernel,
        out_shape=jax.ShapeDtypeStruct((k2, nv, ns), jnp.float32),
        grid=(nv // vt,),
        in_specs=[
            pl.BlockSpec((k2, vt, ns), lambda i: (0, i, 0)),
            pl.BlockSpec((vt, ns), lambda i: (i, 0)),
            pl.BlockSpec((NT, 3 * k2), lambda i: (0, 0)),
            pl.BlockSpec((2 * k2, NT), lambda i: (0, 0)),
        ],
        out_specs=pl.BlockSpec((k2, vt, ns), lambda i: (0, i, 0)),
        cost_estimate=pl.CostEstimate(
            flops=4 * NT * k2 * nv * ns * 3, transcendentals=0, bytes_accessed=(2 * k2 + 1) * nv * ns * 4
        ),
    )(spec, onset_part, fwd3, bwd2)


def product_chunk(reflection, focus_stack, chunk, size):
    vdev = focus_stack.shape[1] // 2
    refl = lax.dynamic_slice_in_dim(reflection, chunk * size, size, axis=2)
    ab = jnp.einsum("fwr,cfsr->fcws", focus_stack, refl, precision=HIGHEST)
    a, b = ab[:, 0], ab[:, 1]
    real = a[:, :vdev] - b[:, vdev:]
    imag = a[:, vdev:] + b[:, :vdev]
    return jnp.stack([real, imag], axis=1)


def adjoint_chunk(reflection, back, chunk):
    fdev, _, vdev, size = back.shape
    stacked = back.reshape(fdev, 2 * vdev, size)
    refl = lax.dynamic_slice_in_dim(reflection, chunk * size, size, axis=2)
    g = jnp.einsum("fws,cfsr->fcwr", stacked, refl, precision=HIGHEST)
    g_r, g_i = g[:, 0], g[:, 1]
    real = g_r[:, :vdev] + g_i[:, vdev:]
    imag = g_r[:, vdev:] - g_i[:, :vdev]
    return jnp.stack([real, imag], axis=1)


def shifted(x, axis, shift, n):
    return lax.ppermute(x, axis, [(i, (i + shift) % n) for i in range(n)])


def window_half(summed, reflection, onset, v0):
    fdev, _, width, own = summed.shape
    n_rcv = lax.axis_size("rcv")
    n_freq = lax.axis_size("freq")
    me_rcv = lax.axis_index("rcv")
    me_freq = lax.axis_index("freq")
    vc = width // n_freq

    spec = jnp.zeros((n_freq, fdev, 2, vc, own), jnp.float32)
    for shift in range(n_freq):
        dest = (me_freq + shift) % n_freq
        block = lax.dynamic_slice_in_dim(summed, dest * vc, vc, axis=2)
        if shift:
            block = shifted(block, "freq", shift, n_freq)
        src = (me_freq - shift) % n_freq
        spec = lax.dynamic_update_index_in_dim(spec, block, src, axis=0)
    fwd3, bwd2 = bases(n_freq, fdev)
    onset_part = lax.dynamic_slice(onset, (v0 + me_freq * vc, me_rcv * own), (vc, own))
    back = window_traces(spec.reshape(n_freq * fdev * 2, vc, own), onset_part, fwd3, bwd2)
    back = back.reshape(n_freq, fdev, 2, vc, own)

    back_full = jnp.zeros((fdev, 2, width, own), jnp.float32)
    for shift in range(n_freq):
        piece = lax.dynamic_index_in_dim(back, (me_freq + shift) % n_freq, axis=0, keepdims=False)
        if shift:
            piece = shifted(piece, "freq", shift, n_freq)
        src = (me_freq - shift) % n_freq
        back_full = lax.dynamic_update_slice_in_dim(back_full, piece, src * vc, axis=2)

    adjoint = None
    for shift in range(n_rcv):
        piece = back_full
        if shift:
            piece = shifted(back_full, "rcv", shift, n_rcv)
        term = adjoint_chunk(reflection, piece, (me_rcv - shift) % n_rcv)
        adjoint = term if adjoint is None else adjoint + term
    return adjoint


def per_device(reflection, focus, initial, onset):
    _, fdev, total_src, nrcv_local = reflection.shape
    vdev = focus.shape[2]
    focus_stack = focus.reshape(fdev, 2 * vdev, nrcv_local)
    n_rcv = lax.axis_size("rcv")
    n_freq = lax.axis_size("freq")
    me_rcv = lax.axis_index("rcv")
    own = total_src // n_rcv

    halves = 2 if (vdev // 2) % n_freq == 0 else 1
    width = vdev // halves

    summed = [None] * halves
    for shift in range(n_rcv):
        part = product_chunk(reflection, focus_stack, (me_rcv + shift) % n_rcv, own)
        for h in range(halves):
            piece = part[:, :, h * width:(h + 1) * width]
            if shift:
                piece = shifted(piece, "rcv", shift, n_rcv)
            summed[h] = piece if summed[h] is None else summed[h] + piece
    parts = [window_half(summed[h], reflection, onset, h * width) for h in range(halves)]
    return initial + jnp.concatenate(parts, axis=2)


def solution(mesh):
    return jax.shard_map(
        per_device,
        mesh=mesh,
        in_specs=(
            P("grp", "freq", None, "rcv"),
            P(("grp", "freq"), None, "sub", "rcv"),
            P(("grp", "freq"), None, "sub", "rcv"),
            P(("grp", "sub"), None),
        ),
        out_specs=P(("grp", "freq"), None, "sub", "rcv"),
        check_vma=False,
    )
```

```python
import math

import jax
import jax.numpy as jnp
import numpy as np
from jax import lax
from jax.experimental import pallas as pl
from jax.experimental.pallas import tpu as pltpu
from jax.sharding import PartitionSpec as P

NT = 512
BF16 = jnp.bfloat16


def split(x):
    high = x.astype(BF16)
    return high, (x - high.astype(jnp.float32)).astype(BF16)


HIGHEST = lax.Precision.HIGHEST


def dot3(lhs3, rhs):
    r_hi, r_lo = split(rhs)
    stacked = jnp.concatenate([r_hi, r_lo, r_hi], axis=0)
    return jnp.dot(lhs3, stacked, preferred_element_type=jnp.float32)


def bases(n_freq_dev, fdev):
    bins = np.arange(1, n_freq_dev * fdev + 1, dtype=np.int64)
    samples = np.arange(NT, dtype=np.int64)
    phase = (bins[:, None] * samples[None, :] % NT).astype(np.float64) * (2.0 * math.pi / NT)
    cosine, sine = np.cos(phase), np.sin(phase)
    pair = np.stack([cosine, -sine], axis=1).reshape(n_freq_dev * fdev * 2, NT)
    fwd_hi, fwd_lo = split_np(((2.0 / NT) * pair).astype(np.float32).T)
    bwd_hi, bwd_lo = split_np(pair.astype(np.float32))
    fwd3 = np.concatenate([fwd_hi, fwd_hi, fwd_lo], axis=1)
    bwd2 = np.concatenate([bwd_hi, bwd_lo], axis=0)
    return jnp.asarray(fwd3), jnp.asarray(bwd2)


def split_np(x):
    high = x.astype(BF16)
    return [high, (x - high.astype(np.float32)).astype(BF16)]


def window_kernel(x_ref, onset_ref, fwd_ref, bwd_ref, out_ref):
    k2 = x_ref.shape[0]
    fwd = fwd_ref[...]
    bwd = bwd_ref[...]
    bwd_hi = bwd_ref[:k2, :]
    for v in range(x_ref.shape[1]):
        trace = dot3(fwd, x_ref[:, v, :])
        samples = lax.broadcasted_iota(jnp.int32, trace.shape, 0)
        windowed = jnp.where(samples < onset_ref[pl.ds(v, 1), :], trace, jnp.float32(0.0))
        w_hi, w_lo = split(windowed)
        both = jnp.dot(bwd, w_hi, preferred_element_type=jnp.float32)
        cross = jnp.dot(bwd_hi, w_lo, preferred_element_type=jnp.float32)
        out_ref[:, v, :] = both[:k2] + (both[k2:] + cross)


def window_traces(spec, onset_part, fwd3, bwd2):
    k2, nv, ns = spec.shape
    vt = 8 if nv % 8 == 0 else nv
    return pl.pallas_call(
        window_kernel,
        out_shape=jax.ShapeDtypeStruct((k2, nv, ns), jnp.float32),
        grid=(nv // vt,),
        in_specs=[
            pl.BlockSpec((k2, vt, ns), lambda i: (0, i, 0)),
            pl.BlockSpec((vt, ns), lambda i: (i, 0)),
            pl.BlockSpec((NT, 3 * k2), lambda i: (0, 0)),
            pl.BlockSpec((2 * k2, NT), lambda i: (0, 0)),
        ],
        out_specs=pl.BlockSpec((k2, vt, ns), lambda i: (0, i, 0)),
        cost_estimate=pl.CostEstimate(
            flops=4 * NT * k2 * nv * ns * 3, transcendentals=0, bytes_accessed=(2 * k2 + 1) * nv * ns * 4
        ),
    )(spec, onset_part, fwd3, bwd2)


def product_chunk(reflection, focus_stack, chunk, size):
    vdev = focus_stack.shape[1] // 2
    refl = lax.dynamic_slice_in_dim(reflection, chunk * size, size, axis=2)
    ab = jnp.einsum("fwr,cfsr->fcws", focus_stack, refl, precision=HIGHEST)
    a, b = ab[:, 0], ab[:, 1]
    real = a[:, :vdev] - b[:, vdev:]
    imag = a[:, vdev:] + b[:, :vdev]
    return jnp.stack([real, imag], axis=1)


def adjoint_chunk(reflection, back, chunk):
    fdev, _, vdev, size = back.shape
    stacked = back.reshape(fdev, 2 * vdev, size)
    refl = lax.dynamic_slice_in_dim(reflection, chunk * size, size, axis=2)
    g = jnp.einsum("fws,cfsr->fcwr", stacked, refl, precision=HIGHEST)
    g_r, g_i = g[:, 0], g[:, 1]
    real = g_r[:, :vdev] + g_i[:, vdev:]
    imag = g_r[:, vdev:] - g_i[:, :vdev]
    return jnp.stack([real, imag], axis=1)


def shifted(x, axis, shift, n):
    return lax.ppermute(x, axis, [(i, (i + shift) % n) for i in range(n)])


def window_half(summed, reflection, onset, v0):
    fdev, _, width, own = summed.shape
    n_rcv = lax.axis_size("rcv")
    n_freq = lax.axis_size("freq")
    me_rcv = lax.axis_index("rcv")
    me_freq = lax.axis_index("freq")
    vc = width // n_freq

    spec = jnp.zeros((n_freq, fdev, 2, vc, own), jnp.float32)
    for shift in range(n_freq):
        dest = (me_freq + shift) % n_freq
        block = lax.dynamic_slice_in_dim(summed, dest * vc, vc, axis=2)
        if shift:
            block = shifted(block, "freq", shift, n_freq)
        src = (me_freq - shift) % n_freq
        spec = lax.dynamic_update_index_in_dim(spec, block, src, axis=0)
    fwd3, bwd2 = bases(n_freq, fdev)
    onset_part = lax.dynamic_slice(onset, (v0 + me_freq * vc, me_rcv * own), (vc, own))
    back = window_traces(spec.reshape(n_freq * fdev * 2, vc, own), onset_part, fwd3, bwd2)
    back = back.reshape(n_freq, fdev, 2, vc, own)

    back_full = jnp.zeros((fdev, 2, width, own), jnp.float32)
    for shift in range(n_freq):
        piece = lax.dynamic_index_in_dim(back, (me_freq + shift) % n_freq, axis=0, keepdims=False)
        if shift:
            piece = shifted(piece, "freq", shift, n_freq)
        src = (me_freq - shift) % n_freq
        back_full = lax.dynamic_update_slice_in_dim(back_full, piece, src * vc, axis=2)

    adjoint = None
    for shift in range(n_rcv):
        piece = back_full
        if shift:
            piece = shifted(back_full, "rcv", shift, n_rcv)
        term = adjoint_chunk(reflection, piece, (me_rcv - shift) % n_rcv)
        adjoint = term if adjoint is None else adjoint + term
    return adjoint


def per_device(reflection, focus, initial, onset):
    _, fdev, total_src, nrcv_local = reflection.shape
    vdev = focus.shape[2]
    focus_stack = focus.reshape(fdev, 2 * vdev, nrcv_local)
    n_rcv = lax.axis_size("rcv")
    n_freq = lax.axis_size("freq")
    me_rcv = lax.axis_index("rcv")
    own = total_src // n_rcv

    halves = 2 if (vdev // 2) % n_freq == 0 else 1
    width = vdev // halves

    summed = [None] * halves
    for shift in range(n_rcv):
        part = product_chunk(reflection, focus_stack, (me_rcv + shift) % n_rcv, own)
        for h in range(halves):
            piece = part[:, :, h * width:(h + 1) * width]
            if shift:
                if h and shift == n_rcv - 1:
                    piece, summed[h - 1] = lax.optimization_barrier((piece, summed[h - 1]))
                piece = shifted(piece, "rcv", shift, n_rcv)
            summed[h] = piece if summed[h] is None else summed[h] + piece
    parts = [window_half(summed[h], reflection, onset, h * width) for h in range(halves)]
    return initial + jnp.concatenate(parts, axis=2)


def solution(mesh):
    return jax.shard_map(
        per_device,
        mesh=mesh,
        in_specs=(
            P("grp", "freq", None, "rcv"),
            P(("grp", "freq"), None, "sub", "rcv"),
            P(("grp", "freq"), None, "sub", "rcv"),
            P(("grp", "sub"), None),
        ),
        out_specs=P(("grp", "freq"), None, "sub", "rcv"),
        check_vma=False,
    )
```

```python
import math

import jax
import jax.numpy as jnp
import numpy as np
from jax import lax
from jax.experimental import pallas as pl
from jax.experimental.pallas import tpu as pltpu
from jax.sharding import PartitionSpec as P

NT = 512
BF16 = jnp.bfloat16


def split(x):
    high = x.astype(BF16)
    return high, (x - high.astype(jnp.float32)).astype(BF16)


HIGHEST = lax.Precision.HIGHEST


def dot3(lhs3, rhs):
    r_hi, r_lo = split(rhs)
    stacked = jnp.concatenate([r_hi, r_lo, r_hi], axis=0)
    return jnp.dot(lhs3, stacked, preferred_element_type=jnp.float32)


def bases(n_freq_dev, fdev):
    bins = np.arange(1, n_freq_dev * fdev + 1, dtype=np.int64)
    samples = np.arange(NT, dtype=np.int64)
    phase = (bins[:, None] * samples[None, :] % NT).astype(np.float64) * (2.0 * math.pi / NT)
    cosine, sine = np.cos(phase), np.sin(phase)
    pair = np.stack([cosine, -sine], axis=1).reshape(n_freq_dev * fdev * 2, NT)
    fwd_hi, fwd_lo = split_np(((2.0 / NT) * pair).astype(np.float32).T)
    bwd_hi, bwd_lo = split_np(pair.astype(np.float32))
    fwd3 = np.concatenate([fwd_hi, fwd_hi, fwd_lo], axis=1)
    bwd2 = np.concatenate([bwd_hi, bwd_lo], axis=0)
    return jnp.asarray(fwd3), jnp.asarray(bwd2)


def split_np(x):
    high = x.astype(BF16)
    return [high, (x - high.astype(np.float32)).astype(BF16)]


def window_kernel(x_ref, onset_ref, fwd_ref, bwd_ref, out_ref):
    k2 = x_ref.shape[0]
    fwd = fwd_ref[...]
    bwd = bwd_ref[...]
    bwd_hi = bwd_ref[:k2, :]
    for v in range(x_ref.shape[1]):
        trace = dot3(fwd, x_ref[:, v, :])
        samples = lax.broadcasted_iota(jnp.int32, trace.shape, 0)
        windowed = jnp.where(samples < onset_ref[pl.ds(v, 1), :], trace, jnp.float32(0.0))
        w_hi, w_lo = split(windowed)
        both = jnp.dot(bwd, w_hi, preferred_element_type=jnp.float32)
        cross = jnp.dot(bwd_hi, w_lo, preferred_element_type=jnp.float32)
        out_ref[:, v, :] = both[:k2] + (both[k2:] + cross)


def window_traces(spec, onset_part, fwd3, bwd2):
    k2, nv, ns = spec.shape
    vt = 8 if nv % 8 == 0 else nv
    return pl.pallas_call(
        window_kernel,
        out_shape=jax.ShapeDtypeStruct((k2, nv, ns), jnp.float32),
        grid=(nv // vt,),
        in_specs=[
            pl.BlockSpec((k2, vt, ns), lambda i: (0, i, 0)),
            pl.BlockSpec((vt, ns), lambda i: (i, 0)),
            pl.BlockSpec((NT, 3 * k2), lambda i: (0, 0)),
            pl.BlockSpec((2 * k2, NT), lambda i: (0, 0)),
        ],
        out_specs=pl.BlockSpec((k2, vt, ns), lambda i: (0, i, 0)),
        cost_estimate=pl.CostEstimate(
            flops=4 * NT * k2 * nv * ns * 3, transcendentals=0, bytes_accessed=(2 * k2 + 1) * nv * ns * 4
        ),
    )(spec, onset_part, fwd3, bwd2)


def product_chunk(reflection, focus_stack, start, size):
    vdev = focus_stack.shape[1] // 2
    refl = lax.dynamic_slice_in_dim(reflection, start, size, axis=2)
    ab = jnp.einsum("fwr,cfsr->fcws", focus_stack, refl, precision=HIGHEST)
    a, b = ab[:, 0], ab[:, 1]
    real = a[:, :vdev] - b[:, vdev:]
    imag = a[:, vdev:] + b[:, :vdev]
    return jnp.stack([real, imag], axis=1)


def adjoint_chunk(reflection, back, chunk):
    fdev, _, vdev, size = back.shape
    stacked = back.reshape(fdev, 2 * vdev, size)
    refl = lax.dynamic_slice_in_dim(reflection, chunk * size, size, axis=2)
    g = jnp.einsum("fws,cfsr->fcwr", stacked, refl, precision=HIGHEST)
    g_r, g_i = g[:, 0], g[:, 1]
    real = g_r[:, :vdev] + g_i[:, vdev:]
    imag = g_r[:, vdev:] - g_i[:, :vdev]
    return jnp.stack([real, imag], axis=1)


def shifted(x, axis, shift, n):
    return lax.ppermute(x, axis, [(i, (i + shift) % n) for i in range(n)])


def window_half(summed, reflection, onset, v0):
    fdev, _, width, own = summed.shape
    n_rcv = lax.axis_size("rcv")
    n_freq = lax.axis_size("freq")
    me_rcv = lax.axis_index("rcv")
    me_freq = lax.axis_index("freq")
    vc = width // n_freq

    spec = jnp.zeros((n_freq, fdev, 2, vc, own), jnp.float32)
    for shift in range(n_freq):
        dest = (me_freq + shift) % n_freq
        block = lax.dynamic_slice_in_dim(summed, dest * vc, vc, axis=2)
        if shift:
            block = shifted(block, "freq", shift, n_freq)
        src = (me_freq - shift) % n_freq
        spec = lax.dynamic_update_index_in_dim(spec, block, src, axis=0)
    fwd3, bwd2 = bases(n_freq, fdev)
    onset_part = lax.dynamic_slice(onset, (v0 + me_freq * vc, me_rcv * own), (vc, own))
    back = window_traces(spec.reshape(n_freq * fdev * 2, vc, own), onset_part, fwd3, bwd2)
    back = back.reshape(n_freq, fdev, 2, vc, own)

    back_full = jnp.zeros((fdev, 2, width, own), jnp.float32)
    for shift in range(n_freq):
        piece = lax.dynamic_index_in_dim(back, (me_freq + shift) % n_freq, axis=0, keepdims=False)
        if shift:
            piece = shifted(piece, "freq", shift, n_freq)
        src = (me_freq - shift) % n_freq
        back_full = lax.dynamic_update_slice_in_dim(back_full, piece, src * vc, axis=2)

    adjoint = None
    for shift in range(n_rcv):
        piece = back_full
        if shift:
            piece = shifted(back_full, "rcv", shift, n_rcv)
        term = adjoint_chunk(reflection, piece, (me_rcv - shift) % n_rcv)
        adjoint = term if adjoint is None else adjoint + term
    return adjoint


def per_device(reflection, focus, initial, onset):
    _, fdev, total_src, nrcv_local = reflection.shape
    vdev = focus.shape[2]
    focus_stack = focus.reshape(fdev, 2 * vdev, nrcv_local)
    n_rcv = lax.axis_size("rcv")
    n_freq = lax.axis_size("freq")
    me_rcv = lax.axis_index("rcv")
    own = total_src // n_rcv

    halves = 2 if (vdev // 2) % n_freq == 0 else 1
    width = vdev // halves

    pieces = 2 if own % 256 == 0 else 1
    step = own // pieces
    received = []
    for shift in range(1, n_rcv):
        dest = (me_rcv + shift) % n_rcv
        sent = []
        for k in range(pieces):
            part = product_chunk(reflection, focus_stack, dest * own + k * step, step)
            sent.append(shifted(part, "rcv", shift, n_rcv))
        received.append(sent[0] if pieces == 1 else jnp.concatenate(sent, axis=3))
    summed = product_chunk(reflection, focus_stack, me_rcv * own, own)
    for part in received:
        summed = summed + part
    parts = [
        window_half(summed[:, :, h * width:(h + 1) * width], reflection, onset, h * width) for h in range(halves)
    ]
    return initial + jnp.concatenate(parts, axis=2)


def solution(mesh):
    return jax.shard_map(
        per_device,
        mesh=mesh,
        in_specs=(
            P("grp", "freq", None, "rcv"),
            P(("grp", "freq"), None, "sub", "rcv"),
            P(("grp", "freq"), None, "sub", "rcv"),
            P(("grp", "sub"), None),
        ),
        out_specs=P(("grp", "freq"), None, "sub", "rcv"),
        check_vma=False,
    )
```

```python
import functools
import math

import jax
import jax.numpy as jnp
import numpy as np
from jax import lax
from jax.experimental import pallas as pl
from jax.experimental.pallas import tpu as pltpu
from jax.sharding import PartitionSpec as P

NT = 512
BF16 = jnp.bfloat16


def split(x):
    high = x.astype(BF16)
    return high, (x - high.astype(jnp.float32)).astype(BF16)


HIGHEST = lax.Precision.HIGHEST


def dot3(lhs3, rhs):
    r_hi, r_lo = split(rhs)
    stacked = jnp.concatenate([r_hi, r_lo, r_hi], axis=0)
    return jnp.dot(lhs3, stacked, preferred_element_type=jnp.float32)


def bases(n_freq_dev, fdev):
    bins = np.arange(1, n_freq_dev * fdev + 1, dtype=np.int64)
    samples = np.arange(NT, dtype=np.int64)
    phase = (bins[:, None] * samples[None, :] % NT).astype(np.float64) * (2.0 * math.pi / NT)
    cosine, sine = np.cos(phase), np.sin(phase)
    pair = np.stack([cosine, -sine], axis=1).reshape(n_freq_dev * fdev * 2, NT)
    fwd_hi, fwd_lo = split_np(((2.0 / NT) * pair).astype(np.float32).T)
    bwd_hi, bwd_lo = split_np(pair.astype(np.float32))
    fwd3 = np.concatenate([fwd_hi, fwd_hi, fwd_lo], axis=1)
    bwd2 = np.concatenate([bwd_hi, bwd_lo], axis=0)
    return jnp.asarray(fwd3), jnp.asarray(bwd2)


def split_np(x):
    high = x.astype(BF16)
    return [high, (x - high.astype(np.float32)).astype(BF16)]


def window_kernel(me_ref, x_ref, onset_ref, fwd_ref, bwd_ref, out_ref, *, block):
    k2 = x_ref.shape[0]
    n_blocks = k2 // block
    me = me_ref[0]
    fwd = fwd_ref[...]
    bwd = bwd_ref[...]
    bwd_hi = bwd_ref[:k2, :]
    for v in range(x_ref.shape[1]):
        trace = dot3(fwd, x_ref[:, v, :])
        samples = lax.broadcasted_iota(jnp.int32, trace.shape, 0)
        windowed = jnp.where(samples < onset_ref[pl.ds(v, 1), :], trace, jnp.float32(0.0))
        w_hi, w_lo = split(windowed)
        both = jnp.dot(bwd, w_hi, preferred_element_type=jnp.float32)
        cross = jnp.dot(bwd_hi, w_lo, preferred_element_type=jnp.float32)
        result = both[:k2] + (both[k2:] + cross)
        for i in range(n_blocks):
            row = pl.multiple_of(lax.rem(i - me + n_blocks, n_blocks) * block, block)
            out_ref[pl.ds(row, block), v, :] = result[i * block:(i + 1) * block]


def window_traces(spec, onset_part, fwd3, bwd2, me, block):
    k2, nv, ns = spec.shape
    vt = 8 if nv % 8 == 0 else nv
    return pl.pallas_call(
        functools.partial(window_kernel, block=block),
        out_shape=jax.ShapeDtypeStruct((k2, nv, ns), jnp.float32),
        grid_spec=pltpu.PrefetchScalarGridSpec(
            num_scalar_prefetch=1,
            grid=(nv // vt,),
            in_specs=[
                pl.BlockSpec((k2, vt, ns), lambda i, m: (0, i, 0)),
                pl.BlockSpec((vt, ns), lambda i, m: (i, 0)),
                pl.BlockSpec((NT, 3 * k2), lambda i, m: (0, 0)),
                pl.BlockSpec((2 * k2, NT), lambda i, m: (0, 0)),
            ],
            out_specs=pl.BlockSpec((k2, vt, ns), lambda i, m: (0, i, 0)),
        ),
        cost_estimate=pl.CostEstimate(
            flops=4 * NT * k2 * nv * ns * 3, transcendentals=0, bytes_accessed=(2 * k2 + 1) * nv * ns * 4
        ),
    )(jnp.reshape(me, (1,)).astype(jnp.int32), spec, onset_part, fwd3, bwd2)


def product_chunk(reflection, focus_stack, start, size):
    vdev = focus_stack.shape[1] // 2
    refl = lax.dynamic_slice_in_dim(reflection, start, size, axis=2)
    ab = jnp.einsum("fwr,cfsr->fcws", focus_stack, refl, precision=HIGHEST)
    a, b = ab[:, 0], ab[:, 1]
    real = a[:, :vdev] - b[:, vdev:]
    imag = a[:, vdev:] + b[:, :vdev]
    return jnp.stack([real, imag], axis=1)


def adjoint_chunk(reflection, back, chunk):
    fdev, _, vdev, size = back.shape
    stacked = back.reshape(fdev, 2 * vdev, size)
    refl = lax.dynamic_slice_in_dim(reflection, chunk * size, size, axis=2)
    g = jnp.einsum("fws,cfsr->fcwr", stacked, refl, precision=HIGHEST)
    g_r, g_i = g[:, 0], g[:, 1]
    real = g_r[:, :vdev] + g_i[:, vdev:]
    imag = g_r[:, vdev:] - g_i[:, :vdev]
    return jnp.stack([real, imag], axis=1)


def shifted(x, axis, shift, n):
    return lax.ppermute(x, axis, [(i, (i + shift) % n) for i in range(n)])


def window_half(summed, reflection, onset, v0):
    fdev, _, width, own = summed.shape
    n_rcv = lax.axis_size("rcv")
    n_freq = lax.axis_size("freq")
    me_rcv = lax.axis_index("rcv")
    me_freq = lax.axis_index("freq")
    vc = width // n_freq

    spec = jnp.zeros((n_freq, fdev, 2, vc, own), jnp.float32)
    for shift in range(n_freq):
        dest = (me_freq + shift) % n_freq
        block = lax.dynamic_slice_in_dim(summed, dest * vc, vc, axis=2)
        if shift:
            block = shifted(block, "freq", shift, n_freq)
        src = (me_freq - shift) % n_freq
        spec = lax.dynamic_update_index_in_dim(spec, block, src, axis=0)
    fwd3, bwd2 = bases(n_freq, fdev)
    onset_part = lax.dynamic_slice(onset, (v0 + me_freq * vc, me_rcv * own), (vc, own))
    back = window_traces(spec.reshape(n_freq * fdev * 2, vc, own), onset_part, fwd3, bwd2, me_freq, fdev * 2)
    back = back.reshape(n_freq, fdev, 2, vc, own)

    back_full = jnp.zeros((fdev, 2, width, own), jnp.float32)
    for shift in range(n_freq):
        piece = back[shift]
        if shift:
            piece = shifted(piece, "freq", shift, n_freq)
        src = (me_freq - shift) % n_freq
        back_full = lax.dynamic_update_slice_in_dim(back_full, piece, src * vc, axis=2)

    adjoint = None
    for shift in range(n_rcv):
        piece = back_full
        if shift:
            piece = shifted(back_full, "rcv", shift, n_rcv)
        term = adjoint_chunk(reflection, piece, (me_rcv - shift) % n_rcv)
        adjoint = term if adjoint is None else adjoint + term
    return adjoint


def per_device(reflection, focus, initial, onset):
    _, fdev, total_src, nrcv_local = reflection.shape
    vdev = focus.shape[2]
    focus_stack = focus.reshape(fdev, 2 * vdev, nrcv_local)
    n_rcv = lax.axis_size("rcv")
    n_freq = lax.axis_size("freq")
    me_rcv = lax.axis_index("rcv")
    own = total_src // n_rcv

    halves = 2 if (vdev // 2) % n_freq == 0 else 1
    width = vdev // halves

    pieces = 2 if own % 256 == 0 else 1
    step = own // pieces
    received = []
    for shift in range(1, n_rcv):
        dest = (me_rcv + shift) % n_rcv
        sent = []
        for k in range(pieces):
            part = product_chunk(reflection, focus_stack, dest * own + k * step, step)
            sent.append(shifted(part, "rcv", shift, n_rcv))
        received.append(sent[0] if pieces == 1 else jnp.concatenate(sent, axis=3))
    summed = product_chunk(reflection, focus_stack, me_rcv * own, own)
    for part in received:
        summed = summed + part
    parts = [
        window_half(summed[:, :, h * width:(h + 1) * width], reflection, onset, h * width) for h in range(halves)
    ]
    return initial + jnp.concatenate(parts, axis=2)


def solution(mesh):
    return jax.shard_map(
        per_device,
        mesh=mesh,
        in_specs=(
            P("grp", "freq", None, "rcv"),
            P(("grp", "freq"), None, "sub", "rcv"),
            P(("grp", "freq"), None, "sub", "rcv"),
            P(("grp", "sub"), None),
        ),
        out_specs=P(("grp", "freq"), None, "sub", "rcv"),
        check_vma=False,
    )
```

```python
import functools
import math

import jax
import jax.numpy as jnp
import numpy as np
from jax import lax
from jax.experimental import pallas as pl
from jax.experimental.pallas import tpu as pltpu
from jax.sharding import PartitionSpec as P

NT = 512
BF16 = jnp.bfloat16


def split(x):
    high = x.astype(BF16)
    return high, (x - high.astype(jnp.float32)).astype(BF16)


HIGHEST = lax.Precision.HIGHEST


def dot3(lhs3, rhs):
    r_hi, r_lo = split(rhs)
    stacked = jnp.concatenate([r_hi, r_lo, r_hi], axis=0)
    return jnp.dot(lhs3, stacked, preferred_element_type=jnp.float32)


def bases(n_freq_dev, fdev):
    bins = np.arange(1, n_freq_dev * fdev + 1, dtype=np.int64)
    samples = np.arange(NT, dtype=np.int64)
    phase = (bins[:, None] * samples[None, :] % NT).astype(np.float64) * (2.0 * math.pi / NT)
    cosine, sine = np.cos(phase), np.sin(phase)
    pair = np.stack([cosine, -sine], axis=1).reshape(n_freq_dev * fdev * 2, NT)
    fwd_hi, fwd_lo = split_np(((2.0 / NT) * pair).astype(np.float32).T)
    bwd_hi, bwd_lo = split_np(pair.astype(np.float32))
    fwd3 = np.concatenate([fwd_hi, fwd_hi, fwd_lo], axis=1)
    bwd2 = np.concatenate([bwd_hi, bwd_lo], axis=0)
    return jnp.asarray(fwd3), jnp.asarray(bwd2)


def split_np(x):
    high = x.astype(BF16)
    return [high, (x - high.astype(np.float32)).astype(BF16)]


def window_kernel(me_ref, x_ref, onset_ref, fwd_ref, bwd_ref, out_ref, *, block):
    k2 = x_ref.shape[0]
    n_blocks = k2 // block
    me = me_ref[0]
    fwd = fwd_ref[...]
    bwd = bwd_ref[...]
    bwd_hi = bwd_ref[:k2, :]
    for v in range(x_ref.shape[1]):
        trace = dot3(fwd, x_ref[:, v, :])
        samples = lax.broadcasted_iota(jnp.int32, trace.shape, 0)
        windowed = jnp.where(samples < onset_ref[pl.ds(v, 1), :], trace, jnp.float32(0.0))
        w_hi, w_lo = split(windowed)
        both = jnp.dot(bwd, w_hi, preferred_element_type=jnp.float32)
        cross = jnp.dot(bwd_hi, w_lo, preferred_element_type=jnp.float32)
        result = both[:k2] + (both[k2:] + cross)
        for i in range(n_blocks):
            row = pl.multiple_of(lax.rem(i - me + n_blocks, n_blocks) * block, block)
            out_ref[pl.ds(row, block), v, :] = result[i * block:(i + 1) * block]


def window_traces(spec, onset_part, fwd3, bwd2, me, block):
    k2, nv, ns = spec.shape
    vt = 8 if nv % 8 == 0 else nv
    return pl.pallas_call(
        functools.partial(window_kernel, block=block),
        out_shape=jax.ShapeDtypeStruct((k2, nv, ns), jnp.float32),
        grid_spec=pltpu.PrefetchScalarGridSpec(
            num_scalar_prefetch=1,
            grid=(nv // vt,),
            in_specs=[
                pl.BlockSpec((k2, vt, ns), lambda i, m: (0, i, 0)),
                pl.BlockSpec((vt, ns), lambda i, m: (i, 0)),
                pl.BlockSpec((NT, 3 * k2), lambda i, m: (0, 0)),
                pl.BlockSpec((2 * k2, NT), lambda i, m: (0, 0)),
            ],
            out_specs=pl.BlockSpec((k2, vt, ns), lambda i, m: (0, i, 0)),
        ),
        cost_estimate=pl.CostEstimate(
            flops=4 * NT * k2 * nv * ns * 3, transcendentals=0, bytes_accessed=(2 * k2 + 1) * nv * ns * 4
        ),
    )(jnp.reshape(me, (1,)).astype(jnp.int32), spec, onset_part, fwd3, bwd2)


def product_chunk(reflection, focus_stack, start, size):
    vdev = focus_stack.shape[1] // 2
    refl = lax.dynamic_slice_in_dim(reflection, start, size, axis=2)
    ab = jnp.einsum("fwr,cfsr->fcws", focus_stack, refl, precision=HIGHEST)
    a, b = ab[:, 0], ab[:, 1]
    real = a[:, :vdev] - b[:, vdev:]
    imag = a[:, vdev:] + b[:, :vdev]
    return jnp.stack([real, imag], axis=1)


def adjoint_chunk(reflection, back, chunk):
    fdev, _, vdev, size = back.shape
    stacked = back.reshape(fdev, 2 * vdev, size)
    refl = lax.dynamic_slice_in_dim(reflection, chunk * size, size, axis=2)
    g = jnp.einsum("fws,cfsr->fcwr", stacked, refl, precision=HIGHEST)
    g_r, g_i = g[:, 0], g[:, 1]
    real = g_r[:, :vdev] + g_i[:, vdev:]
    imag = g_r[:, vdev:] - g_i[:, :vdev]
    return jnp.stack([real, imag], axis=1)


def shifted(x, axis, shift, n):
    return lax.ppermute(x, axis, [(i, (i + shift) % n) for i in range(n)])


def window_half(summed, reflection, onset, v0):
    fdev, _, width, own = summed.shape
    n_rcv = lax.axis_size("rcv")
    n_freq = lax.axis_size("freq")
    me_rcv = lax.axis_index("rcv")
    me_freq = lax.axis_index("freq")
    vc = width // n_freq

    spec = jnp.zeros((n_freq, fdev, 2, vc, own), jnp.float32)
    for shift in range(n_freq):
        dest = (me_freq + shift) % n_freq
        block = lax.dynamic_slice_in_dim(summed, dest * vc, vc, axis=2)
        if shift:
            block = shifted(block, "freq", shift, n_freq)
        src = (me_freq - shift) % n_freq
        spec = lax.dynamic_update_index_in_dim(spec, block, src, axis=0)
    fwd3, bwd2 = bases(n_freq, fdev)
    onset_part = lax.dynamic_slice(onset, (v0 + me_freq * vc, me_rcv * own), (vc, own))
    back = window_traces(spec.reshape(n_freq * fdev * 2, vc, own), onset_part, fwd3, bwd2, me_freq, fdev * 2)
    back = back.reshape(n_freq, fdev, 2, vc, own)

    back_full = jnp.zeros((fdev, 2, width, own), jnp.float32)
    for shift in range(n_freq):
        piece = back[shift]
        if shift:
            piece = shifted(piece, "freq", shift, n_freq)
        src = (me_freq - shift) % n_freq
        back_full = lax.dynamic_update_slice_in_dim(back_full, piece, src * vc, axis=2)

    adjoint = None
    for shift in range(n_rcv):
        piece = back_full
        if shift:
            piece = shifted(back_full, "rcv", shift, n_rcv)
        term = adjoint_chunk(reflection, piece, (me_rcv - shift) % n_rcv)
        adjoint = term if adjoint is None else adjoint + term
    return adjoint


def per_device(reflection, focus, initial, onset):
    _, fdev, total_src, nrcv_local = reflection.shape
    vdev = focus.shape[2]
    focus_stack = focus.reshape(fdev, 2 * vdev, nrcv_local)
    n_rcv = lax.axis_size("rcv")
    n_freq = lax.axis_size("freq")
    me_rcv = lax.axis_index("rcv")
    own = total_src // n_rcv

    halves = 2 if (vdev // 2) % n_freq == 0 else 1
    width = vdev // halves

    pieces = 2 if own % 256 == 0 else 1
    step = own // pieces
    received = []
    for shift in range(1, n_rcv):
        dest = (me_rcv + shift) % n_rcv
        sent = []
        for k in range(pieces):
            part = product_chunk(reflection, focus_stack, dest * own + k * step, step)
            sent.append(shifted(part, "rcv", shift, n_rcv))
        received.append(sent[0] if pieces == 1 else jnp.concatenate(sent, axis=3))
    summed = product_chunk(reflection, focus_stack, me_rcv * own, own)
    for part in received:
        summed = summed + part
    parts = [
        window_half(summed[:, :, h * width:(h + 1) * width], reflection, onset, h * width) for h in range(halves)
    ]
    return jnp.concatenate([initial[:, :, h * width:(h + 1) * width] + parts[h] for h in range(halves)], axis=2)


def solution(mesh):
    return jax.shard_map(
        per_device,
        mesh=mesh,
        in_specs=(
            P("grp", "freq", None, "rcv"),
            P(("grp", "freq"), None, "sub", "rcv"),
            P(("grp", "freq"), None, "sub", "rcv"),
            P(("grp", "sub"), None),
        ),
        out_specs=P(("grp", "freq"), None, "sub", "rcv"),
        check_vma=False,
    )
```

```python
import functools
import math

import jax
import jax.numpy as jnp
import numpy as np
from jax import lax
from jax.experimental import pallas as pl
from jax.experimental.pallas import tpu as pltpu
from jax.sharding import PartitionSpec as P

NT = 512
BF16 = jnp.bfloat16


def split(x):
    high = x.astype(BF16)
    return high, (x - high.astype(jnp.float32)).astype(BF16)


HIGHEST = lax.Precision.HIGHEST


def dot3(lhs3, rhs):
    r_hi, r_lo = split(rhs)
    stacked = jnp.concatenate([r_hi, r_lo, r_hi], axis=0)
    return jnp.dot(lhs3, stacked, preferred_element_type=jnp.float32)


def bases(n_freq_dev, fdev):
    bins = np.arange(1, n_freq_dev * fdev + 1, dtype=np.int64)
    samples = np.arange(NT, dtype=np.int64)
    phase = (bins[:, None] * samples[None, :] % NT).astype(np.float64) * (2.0 * math.pi / NT)
    cosine, sine = np.cos(phase), np.sin(phase)
    pair = np.stack([cosine, -sine], axis=1).reshape(n_freq_dev * fdev * 2, NT)
    fwd_hi, fwd_lo = split_np(((2.0 / NT) * pair).astype(np.float32).T)
    bwd_hi, bwd_lo = split_np(pair.astype(np.float32))
    fwd3 = np.concatenate([fwd_hi, fwd_hi, fwd_lo], axis=1)
    bwd2 = np.concatenate([bwd_hi, bwd_lo], axis=0)
    return jnp.asarray(fwd3), jnp.asarray(bwd2)


def split_np(x):
    high = x.astype(BF16)
    return [high, (x - high.astype(np.float32)).astype(BF16)]


def window_kernel(me_ref, x_ref, onset_ref, fwd_ref, bwd_ref, out_ref, *, block):
    k2 = x_ref.shape[0]
    n_blocks = k2 // block
    me = me_ref[0]
    fwd = fwd_ref[...]
    bwd = bwd_ref[...]
    bwd_hi = bwd_ref[:k2, :]
    nv, ns = x_ref.shape[1], x_ref.shape[2]
    group = 2 if nv % 2 == 0 else 1
    for v0 in range(0, nv, group):
        points = range(v0, v0 + group)
        x = jnp.concatenate([x_ref[:, v, :] for v in points], axis=1)
        onset = jnp.concatenate([onset_ref[pl.ds(v, 1), :] for v in points], axis=1)
        trace = dot3(fwd, x)
        samples = lax.broadcasted_iota(jnp.int32, trace.shape, 0)
        windowed = jnp.where(samples < onset, trace, jnp.float32(0.0))
        w_hi, w_lo = split(windowed)
        both = jnp.dot(bwd, w_hi, preferred_element_type=jnp.float32)
        cross = jnp.dot(bwd_hi, w_lo, preferred_element_type=jnp.float32)
        result = both[:k2] + (both[k2:] + cross)
        for g, v in enumerate(points):
            for i in range(n_blocks):
                row = pl.multiple_of(lax.rem(i - me + n_blocks, n_blocks) * block, block)
                out_ref[pl.ds(row, block), v, :] = result[i * block:(i + 1) * block, g * ns:(g + 1) * ns]


def window_traces(spec, onset_part, fwd3, bwd2, me, block):
    k2, nv, ns = spec.shape
    vt = 8 if nv % 8 == 0 else nv
    return pl.pallas_call(
        functools.partial(window_kernel, block=block),
        out_shape=jax.ShapeDtypeStruct((k2, nv, ns), jnp.float32),
        grid_spec=pltpu.PrefetchScalarGridSpec(
            num_scalar_prefetch=1,
            grid=(nv // vt,),
            in_specs=[
                pl.BlockSpec((k2, vt, ns), lambda i, m: (0, i, 0)),
                pl.BlockSpec((vt, ns), lambda i, m: (i, 0)),
                pl.BlockSpec((NT, 3 * k2), lambda i, m: (0, 0)),
                pl.BlockSpec((2 * k2, NT), lambda i, m: (0, 0)),
            ],
            out_specs=pl.BlockSpec((k2, vt, ns), lambda i, m: (0, i, 0)),
        ),
        cost_estimate=pl.CostEstimate(
            flops=4 * NT * k2 * nv * ns * 3, transcendentals=0, bytes_accessed=(2 * k2 + 1) * nv * ns * 4
        ),
    )(jnp.reshape(me, (1,)).astype(jnp.int32), spec, onset_part, fwd3, bwd2)


def product_chunk(reflection, focus_stack, start, size):
    vdev = focus_stack.shape[1] // 2
    refl = lax.dynamic_slice_in_dim(reflection, start, size, axis=2)
    ab = jnp.einsum("fwr,cfsr->fcws", focus_stack, refl, precision=HIGHEST)
    a, b = ab[:, 0], ab[:, 1]
    real = a[:, :vdev] - b[:, vdev:]
    imag = a[:, vdev:] + b[:, :vdev]
    return jnp.stack([real, imag], axis=1)


def adjoint_chunk(reflection, back, chunk):
    fdev, _, vdev, size = back.shape
    stacked = back.reshape(fdev, 2 * vdev, size)
    refl = lax.dynamic_slice_in_dim(reflection, chunk * size, size, axis=2)
    g = jnp.einsum("fws,cfsr->fcwr", stacked, refl, precision=HIGHEST)
    g_r, g_i = g[:, 0], g[:, 1]
    real = g_r[:, :vdev] + g_i[:, vdev:]
    imag = g_r[:, vdev:] - g_i[:, :vdev]
    return jnp.stack([real, imag], axis=1)


def shifted(x, axis, shift, n):
    return lax.ppermute(x, axis, [(i, (i + shift) % n) for i in range(n)])


def window_half(summed, reflection, onset, v0):
    fdev, _, width, own = summed.shape
    n_rcv = lax.axis_size("rcv")
    n_freq = lax.axis_size("freq")
    me_rcv = lax.axis_index("rcv")
    me_freq = lax.axis_index("freq")
    vc = width // n_freq

    spec = jnp.zeros((n_freq, fdev, 2, vc, own), jnp.float32)
    for shift in range(n_freq):
        dest = (me_freq + shift) % n_freq
        block = lax.dynamic_slice_in_dim(summed, dest * vc, vc, axis=2)
        if shift:
            block = shifted(block, "freq", shift, n_freq)
        src = (me_freq - shift) % n_freq
        spec = lax.dynamic_update_index_in_dim(spec, block, src, axis=0)
    fwd3, bwd2 = bases(n_freq, fdev)
    onset_part = lax.dynamic_slice(onset, (v0 + me_freq * vc, me_rcv * own), (vc, own))
    back = window_traces(spec.reshape(n_freq * fdev * 2, vc, own), onset_part, fwd3, bwd2, me_freq, fdev * 2)
    back = back.reshape(n_freq, fdev, 2, vc, own)

    back_full = jnp.zeros((fdev, 2, width, own), jnp.float32)
    for shift in range(n_freq):
        piece = back[shift]
        if shift:
            piece = shifted(piece, "freq", shift, n_freq)
        src = (me_freq - shift) % n_freq
        back_full = lax.dynamic_update_slice_in_dim(back_full, piece, src * vc, axis=2)

    adjoint = None
    for shift in range(n_rcv):
        piece = back_full
        if shift:
            piece = shifted(back_full, "rcv", shift, n_rcv)
        term = adjoint_chunk(reflection, piece, (me_rcv - shift) % n_rcv)
        adjoint = term if adjoint is None else adjoint + term
    return adjoint


def per_device(reflection, focus, initial, onset):
    _, fdev, total_src, nrcv_local = reflection.shape
    vdev = focus.shape[2]
    focus_stack = focus.reshape(fdev, 2 * vdev, nrcv_local)
    n_rcv = lax.axis_size("rcv")
    n_freq = lax.axis_size("freq")
    me_rcv = lax.axis_index("rcv")
    own = total_src // n_rcv

    halves = 2 if (vdev // 2) % n_freq == 0 else 1
    width = vdev // halves

    pieces = 2 if own % 256 == 0 else 1
    step = own // pieces
    received = []
    for shift in range(1, n_rcv):
        dest = (me_rcv + shift) % n_rcv
        sent = []
        for k in range(pieces):
            part = product_chunk(reflection, focus_stack, dest * own + k * step, step)
            sent.append(shifted(part, "rcv", shift, n_rcv))
        received.append(sent[0] if pieces == 1 else jnp.concatenate(sent, axis=3))
    summed = product_chunk(reflection, focus_stack, me_rcv * own, own)
    for part in received:
        summed = summed + part
    parts = [
        window_half(summed[:, :, h * width:(h + 1) * width], reflection, onset, h * width) for h in range(halves)
    ]
    return initial + jnp.concatenate(parts, axis=2)


def solution(mesh):
    return jax.shard_map(
        per_device,
        mesh=mesh,
        in_specs=(
            P("grp", "freq", None, "rcv"),
            P(("grp", "freq"), None, "sub", "rcv"),
            P(("grp", "freq"), None, "sub", "rcv"),
            P(("grp", "sub"), None),
        ),
        out_specs=P(("grp", "freq"), None, "sub", "rcv"),
        check_vma=False,
    )
```

```python
import functools
import math

import jax
import jax.numpy as jnp
import numpy as np
from jax import lax
from jax.experimental import pallas as pl
from jax.experimental.pallas import tpu as pltpu
from jax.sharding import PartitionSpec as P

NT = 512
BF16 = jnp.bfloat16


def split(x):
    high = x.astype(BF16)
    return high, (x - high.astype(jnp.float32)).astype(BF16)


HIGHEST = lax.Precision.HIGHEST


def dot3(lhs3, rhs):
    r_hi, r_lo = split(rhs)
    stacked = jnp.concatenate([r_hi, r_lo, r_hi], axis=0)
    return jnp.dot(lhs3, stacked, preferred_element_type=jnp.float32)


def bases(n_freq_dev, fdev):
    bins = np.arange(1, n_freq_dev * fdev + 1, dtype=np.int64)
    samples = np.arange(NT, dtype=np.int64)
    phase = (bins[:, None] * samples[None, :] % NT).astype(np.float64) * (2.0 * math.pi / NT)
    cosine, sine = np.cos(phase), np.sin(phase)
    pair = np.stack([cosine, -sine], axis=1).reshape(n_freq_dev * fdev * 2, NT)
    fwd_hi, fwd_lo = split_np(((2.0 / NT) * pair).astype(np.float32).T)
    bwd_hi, bwd_lo = split_np(pair.astype(np.float32))
    fwd3 = np.concatenate([fwd_hi, fwd_hi, fwd_lo], axis=1)
    bwd2 = np.concatenate([bwd_hi, bwd_lo], axis=0)
    return jnp.asarray(fwd3), jnp.asarray(bwd2)


def split_np(x):
    high = x.astype(BF16)
    return [high, (x - high.astype(np.float32)).astype(BF16)]


def window_kernel(me_ref, x_ref, onset_ref, fwd_ref, bwd_ref, out_ref, *, block):
    k2 = x_ref.shape[0]
    n_blocks = k2 // block
    me = me_ref[0]
    fwd = fwd_ref[...]
    bwd = bwd_ref[...]
    bwd_hi = bwd_ref[:k2, :]
    nv, ns = x_ref.shape[1], x_ref.shape[2]
    group = 4 if nv % 4 == 0 else (2 if nv % 2 == 0 else 1)
    for v0 in range(0, nv, group):
        points = range(v0, v0 + group)
        x = jnp.concatenate([x_ref[:, v, :] for v in points], axis=1)
        onset = jnp.concatenate([onset_ref[pl.ds(v, 1), :] for v in points], axis=1)
        trace = dot3(fwd, x)
        samples = lax.broadcasted_iota(jnp.int32, trace.shape, 0)
        windowed = jnp.where(samples < onset, trace, jnp.float32(0.0))
        w_hi, w_lo = split(windowed)
        both = jnp.dot(bwd, w_hi, preferred_element_type=jnp.float32)
        cross = jnp.dot(bwd_hi, w_lo, preferred_element_type=jnp.float32)
        result = both[:k2] + (both[k2:] + cross)
        for g, v in enumerate(points):
            for i in range(n_blocks):
                row = pl.multiple_of(lax.rem(i - me + n_blocks, n_blocks) * block, block)
                out_ref[pl.ds(row, block), v, :] = result[i * block:(i + 1) * block, g * ns:(g + 1) * ns]


def window_traces(spec, onset_part, fwd3, bwd2, me, block):
    k2, nv, ns = spec.shape
    vt = 8 if nv % 8 == 0 else nv
    return pl.pallas_call(
        functools.partial(window_kernel, block=block),
        out_shape=jax.ShapeDtypeStruct((k2, nv, ns), jnp.float32),
        grid_spec=pltpu.PrefetchScalarGridSpec(
            num_scalar_prefetch=1,
            grid=(nv // vt,),
            in_specs=[
                pl.BlockSpec((k2, vt, ns), lambda i, m: (0, i, 0)),
                pl.BlockSpec((vt, ns), lambda i, m: (i, 0)),
                pl.BlockSpec((NT, 3 * k2), lambda i, m: (0, 0)),
                pl.BlockSpec((2 * k2, NT), lambda i, m: (0, 0)),
            ],
            out_specs=pl.BlockSpec((k2, vt, ns), lambda i, m: (0, i, 0)),
        ),
        cost_estimate=pl.CostEstimate(
            flops=4 * NT * k2 * nv * ns * 3, transcendentals=0, bytes_accessed=(2 * k2 + 1) * nv * ns * 4
        ),
    )(jnp.reshape(me, (1,)).astype(jnp.int32), spec, onset_part, fwd3, bwd2)


def product_chunk(reflection, focus_stack, start, size):
    vdev = focus_stack.shape[1] // 2
    refl = lax.dynamic_slice_in_dim(reflection, start, size, axis=2)
    ab = jnp.einsum("fwr,cfsr->fcws", focus_stack, refl, precision=HIGHEST)
    a, b = ab[:, 0], ab[:, 1]
    real = a[:, :vdev] - b[:, vdev:]
    imag = a[:, vdev:] + b[:, :vdev]
    return jnp.stack([real, imag], axis=1)


def adjoint_chunk(reflection, back, chunk):
    fdev, _, vdev, size = back.shape
    stacked = back.reshape(fdev, 2 * vdev, size)
    refl = lax.dynamic_slice_in_dim(reflection, chunk * size, size, axis=2)
    g = jnp.einsum("fws,cfsr->fcwr", stacked, refl, precision=HIGHEST)
    g_r, g_i = g[:, 0], g[:, 1]
    real = g_r[:, :vdev] + g_i[:, vdev:]
    imag = g_r[:, vdev:] - g_i[:, :vdev]
    return jnp.stack([real, imag], axis=1)


def shifted(x, axis, shift, n):
    return lax.ppermute(x, axis, [(i, (i + shift) % n) for i in range(n)])


def window_half(summed, reflection, onset, v0):
    fdev, _, width, own = summed.shape
    n_rcv = lax.axis_size("rcv")
    n_freq = lax.axis_size("freq")
    me_rcv = lax.axis_index("rcv")
    me_freq = lax.axis_index("freq")
    vc = width // n_freq

    spec = jnp.zeros((n_freq, fdev, 2, vc, own), jnp.float32)
    for shift in range(n_freq):
        dest = (me_freq + shift) % n_freq
        block = lax.dynamic_slice_in_dim(summed, dest * vc, vc, axis=2)
        if shift:
            block = shifted(block, "freq", shift, n_freq)
        src = (me_freq - shift) % n_freq
        spec = lax.dynamic_update_index_in_dim(spec, block, src, axis=0)
    fwd3, bwd2 = bases(n_freq, fdev)
    onset_part = lax.dynamic_slice(onset, (v0 + me_freq * vc, me_rcv * own), (vc, own))
    back = window_traces(spec.reshape(n_freq * fdev * 2, vc, own), onset_part, fwd3, bwd2, me_freq, fdev * 2)
    back = back.reshape(n_freq, fdev, 2, vc, own)

    back_full = jnp.zeros((fdev, 2, width, own), jnp.float32)
    for shift in range(n_freq):
        piece = back[shift]
        if shift:
            piece = shifted(piece, "freq", shift, n_freq)
        src = (me_freq - shift) % n_freq
        back_full = lax.dynamic_update_slice_in_dim(back_full, piece, src * vc, axis=2)

    adjoint = None
    for shift in range(n_rcv):
        piece = back_full
        if shift:
            piece = shifted(back_full, "rcv", shift, n_rcv)
        term = adjoint_chunk(reflection, piece, (me_rcv - shift) % n_rcv)
        adjoint = term if adjoint is None else adjoint + term
    return adjoint


def per_device(reflection, focus, initial, onset):
    _, fdev, total_src, nrcv_local = reflection.shape
    vdev = focus.shape[2]
    focus_stack = focus.reshape(fdev, 2 * vdev, nrcv_local)
    n_rcv = lax.axis_size("rcv")
    n_freq = lax.axis_size("freq")
    me_rcv = lax.axis_index("rcv")
    own = total_src // n_rcv

    halves = 2 if (vdev // 2) % n_freq == 0 else 1
    width = vdev // halves

    pieces = 2 if own % 256 == 0 else 1
    step = own // pieces
    received = []
    for shift in range(1, n_rcv):
        dest = (me_rcv + shift) % n_rcv
        sent = []
        for k in range(pieces):
            part = product_chunk(reflection, focus_stack, dest * own + k * step, step)
            sent.append(shifted(part, "rcv", shift, n_rcv))
        received.append(sent[0] if pieces == 1 else jnp.concatenate(sent, axis=3))
    summed = product_chunk(reflection, focus_stack, me_rcv * own, own)
    for part in received:
        summed = summed + part
    parts = [
        window_half(summed[:, :, h * width:(h + 1) * width], reflection, onset, h * width) for h in range(halves)
    ]
    return initial + jnp.concatenate(parts, axis=2)


def solution(mesh):
    return jax.shard_map(
        per_device,
        mesh=mesh,
        in_specs=(
            P("grp", "freq", None, "rcv"),
            P(("grp", "freq"), None, "sub", "rcv"),
            P(("grp", "freq"), None, "sub", "rcv"),
            P(("grp", "sub"), None),
        ),
        out_specs=P(("grp", "freq"), None, "sub", "rcv"),
        check_vma=False,
    )
```

```python
import functools
import math

import jax
import jax.numpy as jnp
import numpy as np
from jax import lax
from jax.experimental import pallas as pl
from jax.experimental.pallas import tpu as pltpu
from jax.sharding import PartitionSpec as P

NT = 512
BF16 = jnp.bfloat16


def split(x):
    high = x.astype(BF16)
    return high, (x - high.astype(jnp.float32)).astype(BF16)


HIGHEST = lax.Precision.HIGHEST


def dot3(lhs3, rhs):
    r_hi, r_lo = split(rhs)
    stacked = jnp.concatenate([r_hi, r_lo, r_hi], axis=0)
    return jnp.dot(lhs3, stacked, preferred_element_type=jnp.float32)


def bases(n_freq_dev, fdev):
    bins = np.arange(1, n_freq_dev * fdev + 1, dtype=np.int64)
    samples = np.arange(NT, dtype=np.int64)
    phase = (bins[:, None] * samples[None, :] % NT).astype(np.float64) * (2.0 * math.pi / NT)
    cosine, sine = np.cos(phase), np.sin(phase)
    pair = np.stack([cosine, -sine], axis=1).reshape(n_freq_dev * fdev * 2, NT)
    fwd_hi, fwd_lo = split_np(((2.0 / NT) * pair).astype(np.float32).T)
    bwd_hi, bwd_lo = split_np(pair.astype(np.float32))
    fwd3 = np.concatenate([fwd_hi, fwd_hi, fwd_lo], axis=1)
    bwd2 = np.concatenate([bwd_hi, bwd_lo], axis=0)
    return jnp.asarray(fwd3), jnp.asarray(bwd2)


def split_np(x):
    high = x.astype(BF16)
    return [high, (x - high.astype(np.float32)).astype(BF16)]


def window_kernel(me_ref, x_ref, onset_ref, fwd_ref, bwd_ref, *refs, block):
    outs, result_ref = refs[:-1], refs[-1]
    k2 = x_ref.shape[0]
    n_blocks = k2 // block
    me = me_ref[0]
    fwd = fwd_ref[...]
    bwd = bwd_ref[...]
    bwd_hi = bwd_ref[:k2, :]
    nv, ns = x_ref.shape[1], x_ref.shape[2]
    group = result_ref.shape[1] // ns
    for v0 in range(0, nv, group):
        points = range(v0, v0 + group)
        x = jnp.concatenate([x_ref[:, v, :] for v in points], axis=1)
        onset = jnp.concatenate([onset_ref[pl.ds(v, 1), :] for v in points], axis=1)
        trace = dot3(fwd, x)
        samples = lax.broadcasted_iota(jnp.int32, trace.shape, 0)
        windowed = jnp.where(samples < onset, trace, jnp.float32(0.0))
        w_hi, w_lo = split(windowed)
        both = jnp.dot(bwd, w_hi, preferred_element_type=jnp.float32)
        cross = jnp.dot(bwd_hi, w_lo, preferred_element_type=jnp.float32)
        result_ref[...] = both[:k2] + (both[k2:] + cross)
        for k in range(n_blocks):
            row = pl.multiple_of(lax.rem(me + k, n_blocks) * block, block)
            rows = result_ref[pl.ds(row, block), :]
            for g, v in enumerate(points):
                outs[k][:, v, :] = rows[:, g * ns:(g + 1) * ns]


def window_traces(spec, onset_part, fwd3, bwd2, me, block):
    k2, nv, ns = spec.shape
    vt = 8 if nv % 8 == 0 else nv
    group = 4 if vt % 4 == 0 else (2 if vt % 2 == 0 else 1)
    n_blocks = k2 // block
    return pl.pallas_call(
        functools.partial(window_kernel, block=block),
        out_shape=[jax.ShapeDtypeStruct((block, nv, ns), jnp.float32)] * n_blocks,
        grid_spec=pltpu.PrefetchScalarGridSpec(
            num_scalar_prefetch=1,
            grid=(nv // vt,),
            in_specs=[
                pl.BlockSpec((k2, vt, ns), lambda i, m: (0, i, 0)),
                pl.BlockSpec((vt, ns), lambda i, m: (i, 0)),
                pl.BlockSpec((NT, 3 * k2), lambda i, m: (0, 0)),
                pl.BlockSpec((2 * k2, NT), lambda i, m: (0, 0)),
            ],
            out_specs=[pl.BlockSpec((block, vt, ns), lambda i, m: (0, i, 0))] * n_blocks,
            scratch_shapes=[pltpu.VMEM((k2, group * ns), jnp.float32)],
        ),
        cost_estimate=pl.CostEstimate(
            flops=4 * NT * k2 * nv * ns * 3, transcendentals=0, bytes_accessed=(2 * k2 + 1) * nv * ns * 4
        ),
    )(jnp.reshape(me, (1,)).astype(jnp.int32), spec, onset_part, fwd3, bwd2)


def product_chunk(reflection, focus_stack, start, size):
    vdev = focus_stack.shape[1] // 2
    refl = lax.dynamic_slice_in_dim(reflection, start, size, axis=2)
    ab = jnp.einsum("fwr,cfsr->fcws", focus_stack, refl, precision=HIGHEST)
    a, b = ab[:, 0], ab[:, 1]
    real = a[:, :vdev] - b[:, vdev:]
    imag = a[:, vdev:] + b[:, :vdev]
    return jnp.stack([real, imag], axis=1)


def adjoint_chunk(reflection, back, chunk):
    fdev, _, vdev, size = back.shape
    stacked = back.reshape(fdev, 2 * vdev, size)
    refl = lax.dynamic_slice_in_dim(reflection, chunk * size, size, axis=2)
    g = jnp.einsum("fws,cfsr->fcwr", stacked, refl, precision=HIGHEST)
    g_r, g_i = g[:, 0], g[:, 1]
    real = g_r[:, :vdev] + g_i[:, vdev:]
    imag = g_r[:, vdev:] - g_i[:, :vdev]
    return jnp.stack([real, imag], axis=1)


def shifted(x, axis, shift, n):
    return lax.ppermute(x, axis, [(i, (i + shift) % n) for i in range(n)])


def window_half(summed, reflection, onset, v0):
    fdev, _, width, own = summed.shape
    n_rcv = lax.axis_size("rcv")
    n_freq = lax.axis_size("freq")
    me_rcv = lax.axis_index("rcv")
    me_freq = lax.axis_index("freq")
    vc = width // n_freq

    spec = jnp.zeros((n_freq, fdev, 2, vc, own), jnp.float32)
    for shift in range(n_freq):
        dest = (me_freq + shift) % n_freq
        block = lax.dynamic_slice_in_dim(summed, dest * vc, vc, axis=2)
        if shift:
            block = shifted(block, "freq", shift, n_freq)
        src = (me_freq - shift) % n_freq
        spec = lax.dynamic_update_index_in_dim(spec, block, src, axis=0)
    fwd3, bwd2 = bases(n_freq, fdev)
    onset_part = lax.dynamic_slice(onset, (v0 + me_freq * vc, me_rcv * own), (vc, own))
    back = window_traces(spec.reshape(n_freq * fdev * 2, vc, own), onset_part, fwd3, bwd2, me_freq, fdev * 2)
    back = [x.reshape(fdev, 2, vc, own) for x in back]

    back_full = jnp.zeros((fdev, 2, width, own), jnp.float32)
    for shift in range(n_freq):
        piece = back[shift]
        if shift:
            piece = shifted(piece, "freq", shift, n_freq)
        src = (me_freq - shift) % n_freq
        back_full = lax.dynamic_update_slice_in_dim(back_full, piece, src * vc, axis=2)

    adjoint = None
    for shift in range(n_rcv):
        piece = back_full
        if shift:
            piece = shifted(back_full, "rcv", shift, n_rcv)
        term = adjoint_chunk(reflection, piece, (me_rcv - shift) % n_rcv)
        adjoint = term if adjoint is None else adjoint + term
    return adjoint


def per_device(reflection, focus, initial, onset):
    _, fdev, total_src, nrcv_local = reflection.shape
    vdev = focus.shape[2]
    focus_stack = focus.reshape(fdev, 2 * vdev, nrcv_local)
    n_rcv = lax.axis_size("rcv")
    n_freq = lax.axis_size("freq")
    me_rcv = lax.axis_index("rcv")
    own = total_src // n_rcv

    halves = 2 if (vdev // 2) % n_freq == 0 else 1
    width = vdev // halves

    pieces = 2 if own % 256 == 0 else 1
    step = own // pieces
    received = []
    for shift in range(1, n_rcv):
        dest = (me_rcv + shift) % n_rcv
        sent = []
        for k in range(pieces):
            part = product_chunk(reflection, focus_stack, dest * own + k * step, step)
            sent.append(shifted(part, "rcv", shift, n_rcv))
        received.append(sent[0] if pieces == 1 else jnp.concatenate(sent, axis=3))
    summed = product_chunk(reflection, focus_stack, me_rcv * own, own)
    for part in received:
        summed = summed + part
    parts = [
        window_half(summed[:, :, h * width:(h + 1) * width], reflection, onset, h * width) for h in range(halves)
    ]
    return initial + jnp.concatenate(parts, axis=2)


def solution(mesh):
    return jax.shard_map(
        per_device,
        mesh=mesh,
        in_specs=(
            P("grp", "freq", None, "rcv"),
            P(("grp", "freq"), None, "sub", "rcv"),
            P(("grp", "freq"), None, "sub", "rcv"),
            P(("grp", "sub"), None),
        ),
        out_specs=P(("grp", "freq"), None, "sub", "rcv"),
        check_vma=False,
    )
```

```python
import functools
import math

import jax
import jax.numpy as jnp
import numpy as np
from jax import lax
from jax.experimental import pallas as pl
from jax.experimental.pallas import tpu as pltpu
from jax.sharding import PartitionSpec as P

NT = 512
BF16 = jnp.bfloat16


def split(x):
    high = x.astype(BF16)
    return high, (x - high.astype(jnp.float32)).astype(BF16)


HIGHEST = lax.Precision.HIGHEST


def dot3(lhs3, rhs):
    r_hi, r_lo = split(rhs)
    stacked = jnp.concatenate([r_hi, r_lo, r_hi], axis=0)
    return jnp.dot(lhs3, stacked, preferred_element_type=jnp.float32)


def bases(n_freq_dev, fdev):
    bins = np.arange(1, n_freq_dev * fdev + 1, dtype=np.int64)
    samples = np.arange(NT, dtype=np.int64)
    phase = (bins[:, None] * samples[None, :] % NT).astype(np.float64) * (2.0 * math.pi / NT)
    cosine, sine = np.cos(phase), np.sin(phase)
    pair = np.stack([cosine, -sine], axis=1).reshape(n_freq_dev * fdev * 2, NT)
    fwd_hi, fwd_lo = split_np(((2.0 / NT) * pair).astype(np.float32).T)
    bwd_hi, bwd_lo = split_np(pair.astype(np.float32))
    fwd3 = np.concatenate([fwd_hi, fwd_hi, fwd_lo], axis=1)
    bwd2 = np.concatenate([bwd_hi, bwd_lo], axis=0)
    return jnp.asarray(fwd3), jnp.asarray(bwd2)


def split_np(x):
    high = x.astype(BF16)
    return [high, (x - high.astype(np.float32)).astype(BF16)]


def window_kernel(me_ref, *refs, block, n_blocks):
    ins, (onset_ref, fwd_ref, bwd_ref) = refs[:n_blocks], refs[n_blocks:n_blocks + 3]
    outs, (x_ref, result_ref) = refs[n_blocks + 3:2 * n_blocks + 3], refs[2 * n_blocks + 3:]
    k2 = x_ref.shape[0]
    me = me_ref[0]
    for k in range(n_blocks):
        row = pl.multiple_of(lax.rem(me - k + n_blocks, n_blocks) * block, block)
        x_ref[pl.ds(row, block), :, :] = ins[k][...]
    fwd = fwd_ref[...]
    bwd = bwd_ref[...]
    bwd_hi = bwd_ref[:k2, :]
    nv, ns = x_ref.shape[1], x_ref.shape[2]
    group = result_ref.shape[1] // ns
    for v0 in range(0, nv, group):
        points = range(v0, v0 + group)
        x = jnp.concatenate([x_ref[:, v, :] for v in points], axis=1)
        onset = jnp.concatenate([onset_ref[pl.ds(v, 1), :] for v in points], axis=1)
        trace = dot3(fwd, x)
        samples = lax.broadcasted_iota(jnp.int32, trace.shape, 0)
        windowed = jnp.where(samples < onset, trace, jnp.float32(0.0))
        w_hi, w_lo = split(windowed)
        both = jnp.dot(bwd, w_hi, preferred_element_type=jnp.float32)
        cross = jnp.dot(bwd_hi, w_lo, preferred_element_type=jnp.float32)
        result_ref[...] = both[:k2] + (both[k2:] + cross)
        for k in range(n_blocks):
            row = pl.multiple_of(lax.rem(me + k, n_blocks) * block, block)
            rows = result_ref[pl.ds(row, block), :]
            for g, v in enumerate(points):
                outs[k][:, v, :] = rows[:, g * ns:(g + 1) * ns]


def window_traces(blocks, onset_part, fwd3, bwd2, me):
    block, nv, ns = blocks[0].shape
    n_blocks = len(blocks)
    k2 = block * n_blocks
    vt = 8 if nv % 8 == 0 else nv
    group = 4 if vt % 4 == 0 else (2 if vt % 2 == 0 else 1)
    return pl.pallas_call(
        functools.partial(window_kernel, block=block, n_blocks=n_blocks),
        out_shape=[jax.ShapeDtypeStruct((block, nv, ns), jnp.float32)] * n_blocks,
        grid_spec=pltpu.PrefetchScalarGridSpec(
            num_scalar_prefetch=1,
            grid=(nv // vt,),
            in_specs=[pl.BlockSpec((block, vt, ns), lambda i, m: (0, i, 0))] * n_blocks + [
                pl.BlockSpec((vt, ns), lambda i, m: (i, 0)),
                pl.BlockSpec((NT, 3 * k2), lambda i, m: (0, 0)),
                pl.BlockSpec((2 * k2, NT), lambda i, m: (0, 0)),
            ],
            out_specs=[pl.BlockSpec((block, vt, ns), lambda i, m: (0, i, 0))] * n_blocks,
            scratch_shapes=[pltpu.VMEM((k2, vt, ns), jnp.float32), pltpu.VMEM((k2, group * ns), jnp.float32)],
        ),
        cost_estimate=pl.CostEstimate(
            flops=4 * NT * k2 * nv * ns * 3, transcendentals=0, bytes_accessed=(2 * k2 + 1) * nv * ns * 4
        ),
    )(jnp.reshape(me, (1,)).astype(jnp.int32), *blocks, onset_part, fwd3, bwd2)


def product_chunk(reflection, focus_stack, start, size):
    vdev = focus_stack.shape[1] // 2
    refl = lax.dynamic_slice_in_dim(reflection, start, size, axis=2)
    ab = jnp.einsum("fwr,cfsr->fcws", focus_stack, refl, precision=HIGHEST)
    a, b = ab[:, 0], ab[:, 1]
    real = a[:, :vdev] - b[:, vdev:]
    imag = a[:, vdev:] + b[:, :vdev]
    return jnp.stack([real, imag], axis=1)


def adjoint_chunk(reflection, back, chunk):
    fdev, _, vdev, size = back.shape
    stacked = back.reshape(fdev, 2 * vdev, size)
    refl = lax.dynamic_slice_in_dim(reflection, chunk * size, size, axis=2)
    g = jnp.einsum("fws,cfsr->fcwr", stacked, refl, precision=HIGHEST)
    g_r, g_i = g[:, 0], g[:, 1]
    real = g_r[:, :vdev] + g_i[:, vdev:]
    imag = g_r[:, vdev:] - g_i[:, :vdev]
    return jnp.stack([real, imag], axis=1)


def shifted(x, axis, shift, n):
    return lax.ppermute(x, axis, [(i, (i + shift) % n) for i in range(n)])


def window_half(summed, reflection, onset, v0):
    fdev, _, width, own = summed.shape
    n_rcv = lax.axis_size("rcv")
    n_freq = lax.axis_size("freq")
    me_rcv = lax.axis_index("rcv")
    me_freq = lax.axis_index("freq")
    vc = width // n_freq

    blocks = []
    for shift in range(n_freq):
        dest = (me_freq + shift) % n_freq
        block = lax.dynamic_slice_in_dim(summed, dest * vc, vc, axis=2)
        if shift:
            block = shifted(block, "freq", shift, n_freq)
        blocks.append(block.reshape(fdev * 2, vc, own))
    fwd3, bwd2 = bases(n_freq, fdev)
    onset_part = lax.dynamic_slice(onset, (v0 + me_freq * vc, me_rcv * own), (vc, own))
    back = window_traces(blocks, onset_part, fwd3, bwd2, me_freq)
    back = [x.reshape(fdev, 2, vc, own) for x in back]

    back_full = jnp.zeros((fdev, 2, width, own), jnp.float32)
    for shift in range(n_freq):
        piece = back[shift]
        if shift:
            piece = shifted(piece, "freq", shift, n_freq)
        src = (me_freq - shift) % n_freq
        back_full = lax.dynamic_update_slice_in_dim(back_full, piece, src * vc, axis=2)

    adjoint = None
    for shift in range(n_rcv):
        piece = back_full
        if shift:
            piece = shifted(back_full, "rcv", shift, n_rcv)
        term = adjoint_chunk(reflection, piece, (me_rcv - shift) % n_rcv)
        adjoint = term if adjoint is None else adjoint + term
    return adjoint


def per_device(reflection, focus, initial, onset):
    _, fdev, total_src, nrcv_local = reflection.shape
    vdev = focus.shape[2]
    focus_stack = focus.reshape(fdev, 2 * vdev, nrcv_local)
    n_rcv = lax.axis_size("rcv")
    n_freq = lax.axis_size("freq")
    me_rcv = lax.axis_index("rcv")
    own = total_src // n_rcv

    halves = 2 if (vdev // 2) % n_freq == 0 else 1
    width = vdev // halves

    pieces = 2 if own % 256 == 0 else 1
    step = own // pieces
    received = []
    for shift in range(1, n_rcv):
        dest = (me_rcv + shift) % n_rcv
        sent = []
        for k in range(pieces):
            part = product_chunk(reflection, focus_stack, dest * own + k * step, step)
            sent.append(shifted(part, "rcv", shift, n_rcv))
        received.append(sent[0] if pieces == 1 else jnp.concatenate(sent, axis=3))
    summed = product_chunk(reflection, focus_stack, me_rcv * own, own)
    for part in received:
        summed = summed + part
    parts = [
        window_half(summed[:, :, h * width:(h + 1) * width], reflection, onset, h * width) for h in range(halves)
    ]
    return initial + jnp.concatenate(parts, axis=2)


def solution(mesh):
    return jax.shard_map(
        per_device,
        mesh=mesh,
        in_specs=(
            P("grp", "freq", None, "rcv"),
            P(("grp", "freq"), None, "sub", "rcv"),
            P(("grp", "freq"), None, "sub", "rcv"),
            P(("grp", "sub"), None),
        ),
        out_specs=P(("grp", "freq"), None, "sub", "rcv"),
        check_vma=False,
    )
```

```python
import functools
import math

import jax
import jax.numpy as jnp
import numpy as np
from jax import lax
from jax.experimental import pallas as pl
from jax.experimental.pallas import tpu as pltpu
from jax.sharding import PartitionSpec as P

NT = 512
BF16 = jnp.bfloat16


def split(x):
    high = x.astype(BF16)
    return high, (x - high.astype(jnp.float32)).astype(BF16)


HIGHEST = lax.Precision.HIGHEST


def dot3(lhs3, rhs):
    r_hi, r_lo = split(rhs)
    stacked = jnp.concatenate([r_hi, r_lo, r_hi], axis=0)
    return jnp.dot(lhs3, stacked, preferred_element_type=jnp.float32)


def bases(n_freq_dev, fdev):
    bins = np.arange(1, n_freq_dev * fdev + 1, dtype=np.int64)
    samples = np.arange(NT, dtype=np.int64)
    phase = (bins[:, None] * samples[None, :] % NT).astype(np.float64) * (2.0 * math.pi / NT)
    cosine, sine = np.cos(phase), np.sin(phase)
    pair = np.stack([cosine, -sine], axis=1).reshape(n_freq_dev * fdev * 2, NT)
    fwd_hi, fwd_lo = split_np(((2.0 / NT) * pair).astype(np.float32).T)
    bwd_hi, bwd_lo = split_np(pair.astype(np.float32))
    fwd3 = np.concatenate([fwd_hi, fwd_hi, fwd_lo], axis=1)
    bwd2 = np.concatenate([bwd_hi, bwd_lo], axis=0)
    return jnp.asarray(fwd3), jnp.asarray(bwd2)


def split_np(x):
    high = x.astype(BF16)
    return [high, (x - high.astype(np.float32)).astype(BF16)]


def window_kernel(me_ref, x_ref, onset_ref, fwd_ref, bwd_ref, *refs, block):
    outs, result_ref = refs[:-1], refs[-1]
    k2 = x_ref.shape[0]
    n_blocks = k2 // block
    me = me_ref[0]
    fwd = fwd_ref[...]
    bwd = bwd_ref[...]
    bwd_hi = bwd_ref[:k2, :]
    nv, ns = x_ref.shape[1], x_ref.shape[2]
    group = result_ref.shape[1] // ns
    for v0 in range(0, nv, group):
        points = range(v0, v0 + group)
        x = jnp.concatenate([x_ref[:, v, :] for v in points], axis=1)
        onset = jnp.concatenate([onset_ref[pl.ds(v, 1), :] for v in points], axis=1)
        trace = dot3(fwd, x)
        samples = lax.broadcasted_iota(jnp.int32, trace.shape, 0)
        windowed = jnp.where(samples < onset, trace, jnp.float32(0.0))
        w_hi, w_lo = split(windowed)
        both = jnp.dot(bwd, w_hi, preferred_element_type=jnp.float32)
        cross = jnp.dot(bwd_hi, w_lo, preferred_element_type=jnp.float32)
        result_ref[...] = both[:k2] + (both[k2:] + cross)
        for k in range(n_blocks):
            row = pl.multiple_of(lax.rem(me + k, n_blocks) * block, block)
            rows = result_ref[pl.ds(row, block), :]
            for g, v in enumerate(points):
                outs[k][:, v, :] = rows[:, g * ns:(g + 1) * ns]


def window_traces(spec, onset_part, fwd3, bwd2, me, block):
    k2, nv, ns = spec.shape
    vt = 8 if nv % 8 == 0 else nv
    group = 8 if vt % 8 == 0 else (4 if vt % 4 == 0 else (2 if vt % 2 == 0 else 1))
    n_blocks = k2 // block
    return pl.pallas_call(
        functools.partial(window_kernel, block=block),
        out_shape=[jax.ShapeDtypeStruct((block, nv, ns), jnp.float32)] * n_blocks,
        grid_spec=pltpu.PrefetchScalarGridSpec(
            num_scalar_prefetch=1,
            grid=(nv // vt,),
            in_specs=[
                pl.BlockSpec((k2, vt, ns), lambda i, m: (0, i, 0)),
                pl.BlockSpec((vt, ns), lambda i, m: (i, 0)),
                pl.BlockSpec((NT, 3 * k2), lambda i, m: (0, 0)),
                pl.BlockSpec((2 * k2, NT), lambda i, m: (0, 0)),
            ],
            out_specs=[pl.BlockSpec((block, vt, ns), lambda i, m: (0, i, 0))] * n_blocks,
            scratch_shapes=[pltpu.VMEM((k2, group * ns), jnp.float32)],
        ),
        cost_estimate=pl.CostEstimate(
            flops=4 * NT * k2 * nv * ns * 3, transcendentals=0, bytes_accessed=(2 * k2 + 1) * nv * ns * 4
        ),
    )(jnp.reshape(me, (1,)).astype(jnp.int32), spec, onset_part, fwd3, bwd2)


def product_chunk(reflection, focus_stack, start, size):
    vdev = focus_stack.shape[1] // 2
    refl = lax.dynamic_slice_in_dim(reflection, start, size, axis=2)
    ab = jnp.einsum("fwr,cfsr->fcws", focus_stack, refl, precision=HIGHEST)
    a, b = ab[:, 0], ab[:, 1]
    real = a[:, :vdev] - b[:, vdev:]
    imag = a[:, vdev:] + b[:, :vdev]
    return jnp.stack([real, imag], axis=1)


def adjoint_chunk(reflection, back, chunk):
    fdev, _, vdev, size = back.shape
    stacked = back.reshape(fdev, 2 * vdev, size)
    refl = lax.dynamic_slice_in_dim(reflection, chunk * size, size, axis=2)
    g = jnp.einsum("fws,cfsr->fcwr", stacked, refl, precision=HIGHEST)
    g_r, g_i = g[:, 0], g[:, 1]
    real = g_r[:, :vdev] + g_i[:, vdev:]
    imag = g_r[:, vdev:] - g_i[:, :vdev]
    return jnp.stack([real, imag], axis=1)


def shifted(x, axis, shift, n):
    return lax.ppermute(x, axis, [(i, (i + shift) % n) for i in range(n)])


def window_half(summed, reflection, onset, v0):
    fdev, _, width, own = summed.shape
    n_rcv = lax.axis_size("rcv")
    n_freq = lax.axis_size("freq")
    me_rcv = lax.axis_index("rcv")
    me_freq = lax.axis_index("freq")
    vc = width // n_freq

    spec = jnp.zeros((n_freq, fdev, 2, vc, own), jnp.float32)
    for shift in range(n_freq):
        dest = (me_freq + shift) % n_freq
        block = lax.dynamic_slice_in_dim(summed, dest * vc, vc, axis=2)
        if shift:
            block = shifted(block, "freq", shift, n_freq)
        src = (me_freq - shift) % n_freq
        spec = lax.dynamic_update_index_in_dim(spec, block, src, axis=0)
    fwd3, bwd2 = bases(n_freq, fdev)
    onset_part = lax.dynamic_slice(onset, (v0 + me_freq * vc, me_rcv * own), (vc, own))
    back = window_traces(spec.reshape(n_freq * fdev * 2, vc, own), onset_part, fwd3, bwd2, me_freq, fdev * 2)
    back = [x.reshape(fdev, 2, vc, own) for x in back]

    back_full = jnp.zeros((fdev, 2, width, own), jnp.float32)
    for shift in range(n_freq):
        piece = back[shift]
        if shift:
            piece = shifted(piece, "freq", shift, n_freq)
        src = (me_freq - shift) % n_freq
        back_full = lax.dynamic_update_slice_in_dim(back_full, piece, src * vc, axis=2)

    adjoint = None
    for shift in range(n_rcv):
        piece = back_full
        if shift:
            piece = shifted(back_full, "rcv", shift, n_rcv)
        term = adjoint_chunk(reflection, piece, (me_rcv - shift) % n_rcv)
        adjoint = term if adjoint is None else adjoint + term
    return adjoint


def per_device(reflection, focus, initial, onset):
    _, fdev, total_src, nrcv_local = reflection.shape
    vdev = focus.shape[2]
    focus_stack = focus.reshape(fdev, 2 * vdev, nrcv_local)
    n_rcv = lax.axis_size("rcv")
    n_freq = lax.axis_size("freq")
    me_rcv = lax.axis_index("rcv")
    own = total_src // n_rcv

    halves = 2 if (vdev // 2) % n_freq == 0 else 1
    width = vdev // halves

    pieces = 2 if own % 256 == 0 else 1
    step = own // pieces
    received = []
    for shift in range(1, n_rcv):
        dest = (me_rcv + shift) % n_rcv
        sent = []
        for k in range(pieces):
            part = product_chunk(reflection, focus_stack, dest * own + k * step, step)
            sent.append(shifted(part, "rcv", shift, n_rcv))
        received.append(sent[0] if pieces == 1 else jnp.concatenate(sent, axis=3))
    summed = product_chunk(reflection, focus_stack, me_rcv * own, own)
    for part in received:
        summed = summed + part
    parts = [
        window_half(summed[:, :, h * width:(h + 1) * width], reflection, onset, h * width) for h in range(halves)
    ]
    return initial + jnp.concatenate(parts, axis=2)


def solution(mesh):
    return jax.shard_map(
        per_device,
        mesh=mesh,
        in_specs=(
            P("grp", "freq", None, "rcv"),
            P(("grp", "freq"), None, "sub", "rcv"),
            P(("grp", "freq"), None, "sub", "rcv"),
            P(("grp", "sub"), None),
        ),
        out_specs=P(("grp", "freq"), None, "sub", "rcv"),
        check_vma=False,
    )
```
